512 devices in a mesh: space: 64 (over z_lo, x, core), ky: 8 (over z_hi, y).
Axes of the slice: x: 4, y: 4, z: 16 (z_hi: 2, z_lo: 8; z = z_hi * 8 + z_lo), core: 2. Of those that a mesh axis runs over, the one named last changes fastest.
Arguments:
- distribution: float32 [64, 128, 256, 128], P('space', 'ky'), may hold values from 0 to 2
- region: int32 [64, 256], P('space'), may hold values from 0 to 5, as said below
- region_doping: float32 [6], replicated, may hold values from -1 to 2
- region_relax: float32 [6], replicated, may hold values from 0.2 to 1
- equilibrium: float32 [128, 128], P('ky'), may hold values from 0.3 to 3
- kx_speed: float32 [128], replicated, may hold values from 0.1 to 1
- upwind_sign: int32 [128], replicated, may hold values from -1 to 1, as said below
Outputs:
- advanced: float32 [64, 128, 256, 128], P('space', 'ky')
The draws below stay inside these ranges and needn't reach their ends.
Inputs may be any that keep to these rules, and one draw needn't show every extreme that they name: region[x, y] = 2 band(y) + m[x, y], with m[x, y] 0 or 1 and band(y) = 0, 1, 2 on three runs of columns, each run at least 32 columns long. `upwind_sign`: exactly 64 entries are 1 and the others -1.
All inputs are finite; a program needn't handle non-finite values.
Results may differ from the reference program's by a relative error of at most 0.0003.
Values sent between devices are 32-bit elements; how exact they have to be, the bound alone decides.
No kernel may reach another device: no remote copies, remote signals or barrier semaphores. Data moves between devices by JAX's collectives and lax.ppermute only.
A program may use at most 64 MiB of HBM per device.

```python
import math
import jax
import jax.numpy as jnp
from jax import lax

NY = 256
KX = 128
KY = 128
REGIONS = 6
NX = 64


def draw_region(key, part):
    first_key, second_key, third_key = jax.random.split(key, 3)
    lower = jax.random.randint(first_key, (), NY // 8, 3 * NY // 8)
    upper = jax.random.randint(second_key, (), 5 * NY // 8, 7 * NY // 8)
    column = jnp.arange(NY, dtype=jnp.int32)
    band_index = (column >= lower).astype(jnp.int32) + (column >= upper).astype(jnp.int32)
    material = jax.random.randint(third_key, (NX, NY), 0, 2)
    return (2 * band_index[None, :] + material).astype(jnp.int32)


def draw_upwind_sign(key, part):
    ordering = jax.random.permutation(key, KX)
    return jnp.where(ordering < KX // 2, 1, -1).astype(jnp.int32)


def block_scale(own_key, extent, shards, least, largest):
    loudness = 1.0
    for dim, shards_of in shards:
        steps = jax.random.uniform(jax.random.fold_in(jax.random.fold_in(own_key, 6), dim), (shards_of,), jnp.float32, least / len(shards), largest / len(shards))
        loudness = loudness * jnp.repeat(jnp.exp(steps), extent[dim] // shards_of).reshape((-1,) + (1,) * (len(extent) - 1 - dim))
    return loudness


def setup_inputs(seed: int = 0) -> dict:
    key_of = jax.random.split(jax.random.key(seed), 8)
    return {
        "distribution": jnp.clip(2.0 * jax.random.uniform(key_of[0], (NX, KY, NY, KX), jnp.float32) ** block_scale(key_of[0], (NX, KY, NY, KX), ((0, 64), (1, 8)), -0.2, 0.2), 0.0, 2.0),
        "region": draw_region(jax.random.fold_in(key_of[7], 71), 0),
        "region_doping": jnp.clip(jax.random.uniform(key_of[2], (REGIONS,), jnp.float32, -1.0, 2.0), -1.0, 2.0),
        "region_relax": jnp.clip(jnp.exp(jax.random.uniform(key_of[3], (REGIONS,), jnp.float32, math.log(0.2), math.log(1.0))), 0.2, 1.0),
        "equilibrium": jnp.clip(jnp.exp(math.log(3.0) - 2.3025851 * jax.random.uniform(key_of[4], (KY, KX), jnp.float32) ** block_scale(key_of[4], (KY, KX), ((0, 8),), -0.2, 0.2)), 0.3, 3.0),
        "kx_speed": jnp.clip(jnp.exp(jax.random.uniform(key_of[5], (KX,), jnp.float32, math.log(0.1), math.log(1.0))), 0.1, 1.0),
        "upwind_sign": draw_upwind_sign(jax.random.fold_in(key_of[7], 71), 0),
    }


COUPLING = 0.04
POISSON = 0.1
STEP = 0.4
DRIFT_Y = 0.8

def sine_table(length):
    positions = jnp.arange(1, length + 1, dtype=jnp.int32)
    phase_index = positions[:, None] * positions[None, :] % (2 * length + 2)
    return jnp.sqrt(2.0 / (length + 1.0)) * jnp.sin(math.pi * phase_index.astype(jnp.float32) / (length + 1.0))

def eigen_values(length):
    positions = jnp.arange(1, length + 1, dtype=jnp.int32).astype(jnp.float32)
    return 4.0 * jnp.sin(0.5 * math.pi * positions / (length + 1.0)) ** 2

def wigner_tables(modes):
    half_count = modes // 2
    shifts = jnp.arange(1, half_count + 1, dtype=jnp.int32)
    wave_index = jnp.arange(modes, dtype=jnp.int32)
    phase_index = shifts[:, None] * wave_index[None, :] % modes
    angles = 2.0 * math.pi / modes * phase_index.astype(jnp.float32)
    forward = jnp.concatenate([jnp.cos(angles), jnp.sin(angles)], axis=0)
    backward = jnp.concatenate([jnp.sin(angles).T, -jnp.cos(angles).T], axis=1)
    return (forward, backward)

def differences(potential, modes):
    half_count = modes // 2
    col_count = potential.shape[1]
    padded = jnp.pad(potential, ((0, 0), (half_count, half_count)))
    shifts = jnp.arange(1, half_count + 1, dtype=jnp.int32)
    column = jnp.arange(col_count, dtype=jnp.int32)
    ahead_vals = padded[:, half_count + column[None, :] + shifts[:, None]]
    behind = padded[:, half_count + column[None, :] - shifts[:, None]]
    return COUPLING * (ahead_vals - behind)

def lookup(region, values_table):
    classes = jnp.arange(values_table.shape[0], dtype=jnp.int32)
    return lax.optimization_barrier(jnp.sum(jnp.where(region[..., None] == classes, values_table, 0.0), axis=-1))

def reference(distribution, region, region_doping, region_relax, equilibrium, kx_speed, upwind_sign):
    precise = lax.Precision.HIGHEST
    row_count, ky_count, col_count, kx_count = distribution.shape
    density = lax.optimization_barrier(jnp.sum(distribution, axis=(1, 3))) / (ky_count * kx_count)
    doping = lookup(region, region_doping)
    relax_rate = lookup(region, region_relax)
    charge = density - doping
    sine_rows = sine_table(row_count)
    sine_cols = sine_table(col_count)
    spectral = jnp.dot(jnp.dot(sine_rows, charge, precision=precise), sine_cols, precision=precise)
    spectral = spectral / (eigen_values(row_count)[:, None] + eigen_values(col_count)[None, :])
    potential = POISSON * jnp.dot(jnp.dot(sine_rows, spectral, precision=precise), sine_cols, precision=precise)
    difference = differences(potential, ky_count)
    forward, backward = wigner_tables(ky_count)
    positive_kx = upwind_sign > 0
    ky_global = jnp.arange(ky_count, dtype=jnp.int32)
    upward = ky_global >= ky_count // 2
    vertical = DRIFT_Y * (ky_global.astype(jnp.float32) + 0.5 - 0.5 * ky_count) / (0.5 * ky_count)

    def one_row(inputs):
        position, weights, density_row, relax_row = inputs
        current = lax.dynamic_index_in_dim(distribution, position, 0, keepdims=False)
        before = lax.dynamic_index_in_dim(distribution, jnp.maximum(position - 1, 0), 0, keepdims=False)
        after = lax.dynamic_index_in_dim(distribution, jnp.minimum(position + 1, row_count - 1), 0, keepdims=False)
        before = jnp.where(position > 0, before, 0.0)
        after = jnp.where(position < row_count - 1, after, 0.0)
        upstream_x = jnp.where(positive_kx[None, None, :], before, after)
        drift_x = -kx_speed[None, None, :] * (current - upstream_x)
        zero_col = jnp.zeros_like(current[:, :1])
        from_low = jnp.concatenate([zero_col, current[:, :-1]], axis=1)
        from_high = jnp.concatenate([current[:, 1:], zero_col], axis=1)
        upstream_y = jnp.where(upward[:, None, None], from_low, from_high)
        drift_y = -jnp.abs(vertical)[:, None, None] * (current - upstream_y)
        flattened = current.reshape(ky_count, col_count * kx_count)
        coeffs = jnp.dot(forward, flattened, precision=precise).reshape(ky_count, col_count, kx_count)
        scaled = coeffs * jnp.concatenate([weights, weights], axis=0)[:, :, None]
        wigner = jnp.dot(backward, scaled.reshape(ky_count, col_count * kx_count), precision=precise)
        wigner = wigner.reshape(ky_count, col_count, kx_count)
        relaxation = relax_row[None, :, None] * (density_row[None, :, None] * equilibrium[:, None, :] - current)
        return current + STEP * (drift_x + drift_y + wigner + relaxation)
    positions = jnp.arange(row_count, dtype=jnp.int32)
    return lax.map(one_row, (positions, difference, density, relax_rate))
```

```python
import math

import jax
import jax.numpy as jnp
from jax import lax
from jax.sharding import PartitionSpec as P

COUPLING = 0.04
POISSON = 0.1
STEP = 0.4
DRIFT_Y = 0.8


def sine_table(length):
    positions = jnp.arange(1, length + 1, dtype=jnp.int32)
    phase_index = positions[:, None] * positions[None, :] % (2 * length + 2)
    return jnp.sqrt(2.0 / (length + 1.0)) * jnp.sin(
        math.pi * phase_index.astype(jnp.float32) / (length + 1.0)
    )


def eigen_values(length):
    positions = jnp.arange(1, length + 1, dtype=jnp.int32).astype(jnp.float32)
    return 4.0 * jnp.sin(0.5 * math.pi * positions / (length + 1.0)) ** 2


def wigner_tables(modes):
    half_count = modes // 2
    shifts = jnp.arange(1, half_count + 1, dtype=jnp.int32)
    wave_index = jnp.arange(modes, dtype=jnp.int32)
    phase_index = shifts[:, None] * wave_index[None, :] % modes
    angles = 2.0 * math.pi / modes * phase_index.astype(jnp.float32)
    forward = jnp.concatenate([jnp.cos(angles), jnp.sin(angles)], axis=0)
    backward = jnp.concatenate([jnp.sin(angles).T, -jnp.cos(angles).T], axis=1)
    return (forward, backward)


def own_differences(potential, modes, first_col, local_cols):
    half_count = modes // 2
    padded = jnp.pad(potential, ((0, 0), (half_count, half_count)))
    window = lax.dynamic_slice_in_dim(padded, first_col, local_cols + 2 * half_count, 1)
    pieces = []
    for offset in range(1, half_count + 1):
        ahead_vals = window[:, half_count + offset : half_count + offset + local_cols]
        behind = window[:, half_count - offset : half_count - offset + local_cols]
        pieces.append(ahead_vals - behind)
    return COUPLING * jnp.stack(pieces, axis=1)


def lookup(region, values_table):
    classes = jnp.arange(values_table.shape[0], dtype=jnp.int32)
    return jnp.sum(jnp.where(region[..., None] == classes, values_table, 0.0), axis=-1)


def xor_pairs(count, bit):
    return [(i, i ^ bit) for i in range(count)]


def sum_over(value, axis):
    count = lax.axis_size(axis)
    bit = 1
    while bit < count:
        value = value + lax.ppermute(value, axis, xor_pairs(count, bit))
        bit *= 2
    return value


def gather_rows(value, axis):
    count = lax.axis_size(axis)
    index = lax.axis_index(axis)
    bit, level = 1, 0
    while bit < count:
        other = lax.ppermute(value, axis, xor_pairs(count, bit))
        low = ((index >> level) & 1) == 0
        value = jnp.where(
            low, jnp.concatenate([value, other], 0), jnp.concatenate([other, value], 0)
        )
        bit *= 2
        level += 1
    return value


def shards(distribution, region, region_doping, region_relax, equilibrium, kx_speed, upwind_sign):
    precise = lax.Precision.HIGHEST
    triple = lax.Precision.HIGH
    row_count, ky_local, col_count, kx_count = distribution.shape
    ky_count = ky_local * lax.axis_size("ky")
    space_count = lax.axis_size("space")
    grid_rows = row_count * space_count
    space_index = lax.axis_index("space")
    row_start = space_index * row_count

    partial_value = jnp.sum(distribution, axis=(1, 3)) / (ky_count * kx_count)
    density = sum_over(partial_value, "ky")
    doping = lookup(region, region_doping)
    relax_rate = lookup(region, region_relax)
    charge = density - doping
    every_row = gather_rows(charge, "space")

    sine_rows = sine_table(grid_rows)
    sine_cols = sine_table(col_count)
    eigen_cols = eigen_values(col_count)
    along_x = jnp.dot(sine_rows, every_row, precision=precise)
    spectral = jnp.dot(along_x, sine_cols, precision=precise)
    spectral = spectral / (eigen_values(grid_rows)[:, None] + eigen_cols[None, :])
    back_cols = jnp.dot(spectral, sine_cols, precision=precise)
    own_rows = lax.dynamic_slice_in_dim(sine_rows, row_start, row_count, 0)
    potential = POISSON * jnp.dot(own_rows, back_cols, precision=precise)

    spread = lax.all_to_all(distribution, "ky", split_axis=2, concat_axis=1, tiled=True)
    local_cols = spread.shape[2]
    forward, backward = wigner_tables(ky_count)
    weights = own_differences(potential, ky_count, lax.axis_index("ky") * local_cols, local_cols)
    flattened = spread.reshape(row_count, ky_count, local_cols * kx_count)
    coeffs = jnp.einsum("ab,rbm->ram", forward, flattened, precision=triple)
    coeffs = coeffs.reshape(row_count, ky_count, local_cols, kx_count)
    scaled = coeffs * jnp.concatenate([weights, weights], axis=1)[..., None]
    mixed = jnp.einsum(
        "ab,rbm->ram",
        backward,
        scaled.reshape(row_count, ky_count, local_cols * kx_count),
        precision=triple,
    )
    mixed = mixed.reshape(row_count, ky_count, local_cols, kx_count)
    wigner = lax.all_to_all(mixed, "ky", split_axis=1, concat_axis=2, tiled=True)

    positive_kx = upwind_sign > 0
    half_kx = kx_count // 2
    rank_pos = jnp.cumsum(positive_kx.astype(jnp.int32)) - 1
    rank_neg = jnp.cumsum((~positive_kx).astype(jnp.int32)) - 1
    slots = jnp.arange(half_kx, dtype=jnp.int32)
    pick_pos = (positive_kx[:, None] & (rank_pos[:, None] == slots[None, :])).astype(jnp.float32)
    pick_neg = ((~positive_kx)[:, None] & (rank_neg[:, None] == slots[None, :])).astype(jnp.float32)
    flat = distribution.reshape(-1, kx_count)
    send_right = jnp.dot(flat, pick_pos, precision=precise)
    send_left = jnp.dot(flat, pick_neg, precision=precise)
    forward_pairs = [(i, i + 1) for i in range(space_count - 1)]
    backward_pairs = [(i + 1, i) for i in range(space_count - 1)]
    got_left = lax.ppermute(send_right, "space", forward_pairs)
    got_right = lax.ppermute(send_left, "space", backward_pairs)
    upstream_x = jnp.dot(got_left, pick_pos.T, precision=precise) + jnp.dot(
        got_right, pick_neg.T, precision=precise
    )
    upstream_x = upstream_x.reshape(distribution.shape)
    drift_x = -kx_speed[None, None, None, :] * (distribution - upstream_x)

    ky_global = lax.axis_index("ky") * ky_local + jnp.arange(ky_local, dtype=jnp.int32)
    upward = ky_global >= ky_count // 2
    vertical = DRIFT_Y * (ky_global.astype(jnp.float32) + 0.5 - 0.5 * ky_count) / (0.5 * ky_count)
    zero_col = jnp.zeros_like(distribution[:, :, :1])
    from_low = jnp.concatenate([zero_col, distribution[:, :, :-1]], axis=2)
    from_high = jnp.concatenate([distribution[:, :, 1:], zero_col], axis=2)
    upstream_y = jnp.where(upward[None, :, None, None], from_low, from_high)
    drift_y = -jnp.abs(vertical)[None, :, None, None] * (distribution - upstream_y)
    relaxation = relax_rate[:, None, :, None] * (
        density[:, None, :, None] * equilibrium[None, :, None, :] - distribution
    )
    return distribution + STEP * (drift_x + drift_y + wigner + relaxation)


def solution(mesh):
    return jax.shard_map(
        shards,
        mesh=mesh,
        in_specs=(
            P("space", "ky", None, None),
            P("space", None),
            P(),
            P(),
            P("ky", None),
            P(),
            P(),
        ),
        out_specs=P("space", "ky", None, None),
        check_vma=False,
    )
```

```python
import math

import jax
import jax.numpy as jnp
from jax import lax
from jax.sharding import PartitionSpec as P

COUPLING = 0.04
POISSON = 0.1
STEP = 0.4
DRIFT_Y = 0.8


def sine_table(length):
    positions = jnp.arange(1, length + 1, dtype=jnp.int32)
    phase_index = positions[:, None] * positions[None, :] % (2 * length + 2)
    return jnp.sqrt(2.0 / (length + 1.0)) * jnp.sin(
        math.pi * phase_index.astype(jnp.float32) / (length + 1.0)
    )


def eigen_values(length):
    positions = jnp.arange(1, length + 1, dtype=jnp.int32).astype(jnp.float32)
    return 4.0 * jnp.sin(0.5 * math.pi * positions / (length + 1.0)) ** 2


def wigner_tables(modes):
    half_count = modes // 2
    shifts = jnp.arange(1, half_count + 1, dtype=jnp.int32)
    wave_index = jnp.arange(modes, dtype=jnp.int32)
    phase_index = shifts[:, None] * wave_index[None, :] % modes
    angles = 2.0 * math.pi / modes * phase_index.astype(jnp.float32)
    forward = jnp.concatenate([jnp.cos(angles), jnp.sin(angles)], axis=0)
    backward = jnp.concatenate([jnp.sin(angles).T, -jnp.cos(angles).T], axis=1)
    return (forward, backward)


def own_differences(potential, modes, first_col, local_cols):
    half_count = modes // 2
    padded = jnp.pad(potential, ((0, 0), (half_count, half_count)))
    window = lax.dynamic_slice_in_dim(padded, first_col, local_cols + 2 * half_count, 1)
    pieces = []
    for offset in range(1, half_count + 1):
        ahead_vals = window[:, half_count + offset : half_count + offset + local_cols]
        behind = window[:, half_count - offset : half_count - offset + local_cols]
        pieces.append(ahead_vals - behind)
    return COUPLING * jnp.stack(pieces, axis=1)


def lookup(region, values_table):
    classes = jnp.arange(values_table.shape[0], dtype=jnp.int32)
    return jnp.sum(jnp.where(region[..., None] == classes, values_table, 0.0), axis=-1)


def xor_pairs(count, bit):
    return [(i, i ^ bit) for i in range(count)]


def sum_over(value, axis):
    count = lax.axis_size(axis)
    bit = 1
    while bit < count:
        value = value + lax.ppermute(value, axis, xor_pairs(count, bit))
        bit *= 2
    return value


def gather_rows(value, axis, bits):
    count = lax.axis_size(axis)
    index = lax.axis_index(axis)
    for bit in bits:
        other = lax.ppermute(value, axis, xor_pairs(count, bit))
        low = (index & bit) == 0
        value = jnp.where(
            low, jnp.concatenate([value, other], 0), jnp.concatenate([other, value], 0)
        )
    return value


def in_row_order(value, bits, count):
    levels = len(bits)
    shaped = value.reshape((2,) * levels + (-1,) + value.shape[1:])
    order = sorted(range(levels), key=lambda axis: -bits[levels - 1 - axis])
    shaped = jnp.transpose(shaped, order + list(range(levels, shaped.ndim)))
    return shaped.reshape((count,) + value.shape[1:])


def shards(distribution, region, region_doping, region_relax, equilibrium, kx_speed, upwind_sign):
    precise = lax.Precision.HIGHEST
    triple = lax.Precision.HIGH
    row_count, ky_local, col_count, kx_count = distribution.shape
    ky_count = ky_local * lax.axis_size("ky")
    space_count = lax.axis_size("space")
    grid_rows = row_count * space_count
    space_index = lax.axis_index("space")
    row_start = space_index * row_count

    partial_value = jnp.sum(distribution, axis=(1, 3)) / (ky_count * kx_count)
    density = sum_over(partial_value, "ky")
    doping = lookup(region, region_doping)
    relax_rate = lookup(region, region_relax)
    charge = density - doping
    far_bits = [bit for bit in (8, 16, 32) if bit < space_count]
    near_bits = [bit for bit in (1, 2, 4) if bit < space_count]
    far_rows = gather_rows(charge, "space", far_bits)
    held, far_rows = lax.optimization_barrier((distribution, far_rows))
    every_row = gather_rows(far_rows, "space", near_bits)
    every_row = in_row_order(every_row, far_bits + near_bits, space_count * row_count)

    sine_rows = sine_table(grid_rows)
    sine_cols = sine_table(col_count)
    eigen_cols = eigen_values(col_count)
    along_x = jnp.dot(sine_rows, every_row, precision=precise)
    spectral = jnp.dot(along_x, sine_cols, precision=precise)
    spectral = spectral / (eigen_values(grid_rows)[:, None] + eigen_cols[None, :])
    back_cols = jnp.dot(spectral, sine_cols, precision=precise)
    own_rows = lax.dynamic_slice_in_dim(sine_rows, row_start, row_count, 0)
    potential = POISSON * jnp.dot(own_rows, back_cols, precision=precise)

    spread = lax.all_to_all(held, "ky", split_axis=2, concat_axis=1, tiled=True)
    local_cols = spread.shape[2]
    forward, backward = wigner_tables(ky_count)
    weights = own_differences(potential, ky_count, lax.axis_index("ky") * local_cols, local_cols)
    flattened = spread.reshape(row_count, ky_count, local_cols * kx_count)
    coeffs = jnp.einsum("ab,rbm->ram", forward, flattened, precision=triple)
    coeffs = coeffs.reshape(row_count, ky_count, local_cols, kx_count)
    scaled = coeffs * jnp.concatenate([weights, weights], axis=1)[..., None]
    mixed = jnp.einsum(
        "ab,rbm->ram",
        backward,
        scaled.reshape(row_count, ky_count, local_cols * kx_count),
        precision=triple,
    )
    mixed = mixed.reshape(row_count, ky_count, local_cols, kx_count)
    wigner = lax.all_to_all(mixed, "ky", split_axis=1, concat_axis=2, tiled=True)

    positive_kx = upwind_sign > 0
    half_kx = kx_count // 2
    rank_pos = jnp.cumsum(positive_kx.astype(jnp.int32)) - 1
    rank_neg = jnp.cumsum((~positive_kx).astype(jnp.int32)) - 1
    slots = jnp.arange(half_kx, dtype=jnp.int32)
    pick_pos = (positive_kx[:, None] & (rank_pos[:, None] == slots[None, :])).astype(jnp.float32)
    pick_neg = ((~positive_kx)[:, None] & (rank_neg[:, None] == slots[None, :])).astype(jnp.float32)
    flat = distribution.reshape(-1, kx_count)
    send_right = jnp.dot(flat, pick_pos, precision=precise)
    send_left = jnp.dot(flat, pick_neg, precision=precise)
    forward_pairs = [(i, i + 1) for i in range(space_count - 1)]
    backward_pairs = [(i + 1, i) for i in range(space_count - 1)]
    got_left = lax.ppermute(send_right, "space", forward_pairs)
    got_right = lax.ppermute(send_left, "space", backward_pairs)
    upstream_x = jnp.dot(got_left, pick_pos.T, precision=precise) + jnp.dot(
        got_right, pick_neg.T, precision=precise
    )
    upstream_x = upstream_x.reshape(distribution.shape)
    drift_x = -kx_speed[None, None, None, :] * (distribution - upstream_x)

    ky_global = lax.axis_index("ky") * ky_local + jnp.arange(ky_local, dtype=jnp.int32)
    upward = ky_global >= ky_count // 2
    vertical = DRIFT_Y * (ky_global.astype(jnp.float32) + 0.5 - 0.5 * ky_count) / (0.5 * ky_count)
    zero_col = jnp.zeros_like(distribution[:, :, :1])
    from_low = jnp.concatenate([zero_col, distribution[:, :, :-1]], axis=2)
    from_high = jnp.concatenate([distribution[:, :, 1:], zero_col], axis=2)
    upstream_y = jnp.where(upward[None, :, None, None], from_low, from_high)
    drift_y = -jnp.abs(vertical)[None, :, None, None] * (distribution - upstream_y)
    relaxation = relax_rate[:, None, :, None] * (
        density[:, None, :, None] * equilibrium[None, :, None, :] - distribution
    )
    return distribution + STEP * (drift_x + drift_y + wigner + relaxation)


def solution(mesh):
    return jax.shard_map(
        shards,
        mesh=mesh,
        in_specs=(
            P("space", "ky", None, None),
            P("space", None),
            P(),
            P(),
            P("ky", None),
            P(),
            P(),
        ),
        out_specs=P("space", "ky", None, None),
        check_vma=False,
    )
```

```python
import math

import jax
import jax.numpy as jnp
from jax import lax
from jax.sharding import PartitionSpec as P

COUPLING = 0.04
POISSON = 0.1
STEP = 0.4
DRIFT_Y = 0.8


def sine_table(length):
    positions = jnp.arange(1, length + 1, dtype=jnp.int32)
    phase_index = positions[:, None] * positions[None, :] % (2 * length + 2)
    return jnp.sqrt(2.0 / (length + 1.0)) * jnp.sin(
        math.pi * phase_index.astype(jnp.float32) / (length + 1.0)
    )


def eigen_values(length):
    positions = jnp.arange(1, length + 1, dtype=jnp.int32).astype(jnp.float32)
    return 4.0 * jnp.sin(0.5 * math.pi * positions / (length + 1.0)) ** 2


def wigner_tables(modes):
    half_count = modes // 2
    shifts = jnp.arange(1, half_count + 1, dtype=jnp.int32)
    wave_index = jnp.arange(modes, dtype=jnp.int32)
    phase_index = shifts[:, None] * wave_index[None, :] % modes
    angles = 2.0 * math.pi / modes * phase_index.astype(jnp.float32)
    forward = jnp.concatenate([jnp.cos(angles), jnp.sin(angles)], axis=0)
    backward = jnp.concatenate([jnp.sin(angles).T, -jnp.cos(angles).T], axis=1)
    return (forward, backward)


def own_differences(potential, modes, first_col, local_cols):
    half_count = modes // 2
    padded = jnp.pad(potential, ((0, 0), (half_count, half_count)))
    window = lax.dynamic_slice_in_dim(padded, first_col, local_cols + 2 * half_count, 1)
    pieces = []
    for offset in range(1, half_count + 1):
        ahead_vals = window[:, half_count + offset : half_count + offset + local_cols]
        behind = window[:, half_count - offset : half_count - offset + local_cols]
        pieces.append(ahead_vals - behind)
    return COUPLING * jnp.stack(pieces, axis=1)


def lookup(region, values_table):
    classes = jnp.arange(values_table.shape[0], dtype=jnp.int32)
    return jnp.sum(jnp.where(region[..., None] == classes, values_table, 0.0), axis=-1)


def xor_pairs(count, bit):
    return [(i, i ^ bit) for i in range(count)]


def sum_over(value, axis):
    count = lax.axis_size(axis)
    bit = 1
    while bit < count:
        value = value + lax.ppermute(value, axis, xor_pairs(count, bit))
        bit *= 2
    return value


def gather_rows(value, axis, bits):
    count = lax.axis_size(axis)
    index = lax.axis_index(axis)
    for bit in bits:
        other = lax.ppermute(value, axis, xor_pairs(count, bit))
        low = (index & bit) == 0
        value = jnp.where(
            low, jnp.concatenate([value, other], 0), jnp.concatenate([other, value], 0)
        )
    return value


def in_row_order(value, bits, count):
    levels = len(bits)
    shaped = value.reshape((2,) * levels + (-1,) + value.shape[1:])
    order = sorted(range(levels), key=lambda axis: -bits[levels - 1 - axis])
    shaped = jnp.transpose(shaped, order + list(range(levels, shaped.ndim)))
    return shaped.reshape((count,) + value.shape[1:])


def shards(distribution, region, region_doping, region_relax, equilibrium, kx_speed, upwind_sign):
    precise = lax.Precision.HIGHEST
    triple = lax.Precision.HIGH
    row_count, ky_local, col_count, kx_count = distribution.shape
    ky_count = ky_local * lax.axis_size("ky")
    space_count = lax.axis_size("space")
    grid_rows = row_count * space_count
    space_index = lax.axis_index("space")
    row_start = space_index * row_count

    partial_value = jnp.sum(distribution, axis=(1, 3)) / (ky_count * kx_count)
    density = sum_over(partial_value, "ky")
    doping = lookup(region, region_doping)
    relax_rate = lookup(region, region_relax)
    charge = density - doping
    far_bits = [bit for bit in (8, 16, 32) if bit < space_count]
    near_bits = [bit for bit in (1, 2, 4) if bit < space_count]
    positive_kx = upwind_sign > 0
    half_kx = kx_count // 2
    rank_pos = jnp.cumsum(positive_kx.astype(jnp.int32)) - 1
    rank_neg = jnp.cumsum((~positive_kx).astype(jnp.int32)) - 1
    slots = jnp.arange(half_kx, dtype=jnp.int32)
    pick_pos = (positive_kx[:, None] & (rank_pos[:, None] == slots[None, :])).astype(jnp.float32)
    pick_neg = ((~positive_kx)[:, None] & (rank_neg[:, None] == slots[None, :])).astype(jnp.float32)
    flat = distribution.reshape(-1, kx_count)
    send_right = jnp.dot(flat, pick_pos, precision=precise)
    send_left = jnp.dot(flat, pick_neg, precision=precise)
    forward_pairs = [(i, i + 1) for i in range(space_count - 1)]
    backward_pairs = [(i + 1, i) for i in range(space_count - 1)]
    got_left = lax.ppermute(send_right, "space", forward_pairs)
    got_right = lax.ppermute(send_left, "space", backward_pairs)
    far_rows = gather_rows(charge, "space", far_bits)
    held, far_rows, got_left, got_right = lax.optimization_barrier(
        (distribution, far_rows, got_left, got_right)
    )
    every_row = gather_rows(far_rows, "space", near_bits)
    every_row = in_row_order(every_row, far_bits + near_bits, space_count * row_count)

    sine_rows = sine_table(grid_rows)
    sine_cols = sine_table(col_count)
    eigen_cols = eigen_values(col_count)
    along_x = jnp.dot(sine_rows, every_row, precision=precise)
    spectral = jnp.dot(along_x, sine_cols, precision=precise)
    spectral = spectral / (eigen_values(grid_rows)[:, None] + eigen_cols[None, :])
    back_cols = jnp.dot(spectral, sine_cols, precision=precise)
    own_rows = lax.dynamic_slice_in_dim(sine_rows, row_start, row_count, 0)
    potential = POISSON * jnp.dot(own_rows, back_cols, precision=precise)

    spread = lax.all_to_all(held, "ky", split_axis=2, concat_axis=1, tiled=True)
    local_cols = spread.shape[2]
    forward, backward = wigner_tables(ky_count)
    weights = own_differences(potential, ky_count, lax.axis_index("ky") * local_cols, local_cols)
    flattened = spread.reshape(row_count, ky_count, local_cols * kx_count)
    coeffs = jnp.einsum("ab,rbm->ram", forward, flattened, precision=triple)
    coeffs = coeffs.reshape(row_count, ky_count, local_cols, kx_count)
    scaled = coeffs * jnp.concatenate([weights, weights], axis=1)[..., None]
    mixed = jnp.einsum(
        "ab,rbm->ram",
        backward,
        scaled.reshape(row_count, ky_count, local_cols * kx_count),
        precision=triple,
    )
    mixed = mixed.reshape(row_count, ky_count, local_cols, kx_count)
    wigner = lax.all_to_all(mixed, "ky", split_axis=1, concat_axis=2, tiled=True)

    upstream_x = jnp.dot(got_left, pick_pos.T, precision=precise) + jnp.dot(
        got_right, pick_neg.T, precision=precise
    )
    upstream_x = upstream_x.reshape(distribution.shape)
    drift_x = -kx_speed[None, None, None, :] * (distribution - upstream_x)

    ky_global = lax.axis_index("ky") * ky_local + jnp.arange(ky_local, dtype=jnp.int32)
    upward = ky_global >= ky_count // 2
    vertical = DRIFT_Y * (ky_global.astype(jnp.float32) + 0.5 - 0.5 * ky_count) / (0.5 * ky_count)
    zero_col = jnp.zeros_like(distribution[:, :, :1])
    from_low = jnp.concatenate([zero_col, distribution[:, :, :-1]], axis=2)
    from_high = jnp.concatenate([distribution[:, :, 1:], zero_col], axis=2)
    upstream_y = jnp.where(upward[None, :, None, None], from_low, from_high)
    drift_y = -jnp.abs(vertical)[None, :, None, None] * (distribution - upstream_y)
    relaxation = relax_rate[:, None, :, None] * (
        density[:, None, :, None] * equilibrium[None, :, None, :] - distribution
    )
    return distribution + STEP * (drift_x + drift_y + wigner + relaxation)


def solution(mesh):
    return jax.shard_map(
        shards,
        mesh=mesh,
        in_specs=(
            P("space", "ky", None, None),
            P("space", None),
            P(),
            P(),
            P("ky", None),
            P(),
            P(),
        ),
        out_specs=P("space", "ky", None, None),
        check_vma=False,
    )
```

```python
import math

import jax
import jax.numpy as jnp
from jax import lax
from jax.sharding import PartitionSpec as P

COUPLING = 0.04
POISSON = 0.1
STEP = 0.4
DRIFT_Y = 0.8


def sine_table(length):
    positions = jnp.arange(1, length + 1, dtype=jnp.int32)
    phase_index = positions[:, None] * positions[None, :] % (2 * length + 2)
    return jnp.sqrt(2.0 / (length + 1.0)) * jnp.sin(
        math.pi * phase_index.astype(jnp.float32) / (length + 1.0)
    )


def eigen_values(length):
    positions = jnp.arange(1, length + 1, dtype=jnp.int32).astype(jnp.float32)
    return 4.0 * jnp.sin(0.5 * math.pi * positions / (length + 1.0)) ** 2


def wigner_tables(modes):
    half_count = modes // 2
    shifts = jnp.arange(1, half_count + 1, dtype=jnp.int32)
    wave_index = jnp.arange(modes, dtype=jnp.int32)
    phase_index = shifts[:, None] * wave_index[None, :] % modes
    angles = 2.0 * math.pi / modes * phase_index.astype(jnp.float32)
    forward = jnp.concatenate([jnp.cos(angles), jnp.sin(angles)], axis=0)
    backward = jnp.concatenate([jnp.sin(angles).T, -jnp.cos(angles).T], axis=1)
    return (forward, backward)


def own_differences(potential, modes, first_col, local_cols):
    half_count = modes // 2
    col_count = potential.shape[1]
    source = jnp.arange(col_count, dtype=jnp.int32)[:, None, None]
    shift = jnp.arange(1, half_count + 1, dtype=jnp.int32)[None, :, None]
    column = first_col + jnp.arange(local_cols, dtype=jnp.int32)[None, None, :]
    select = (source == column + shift).astype(jnp.float32) - (source == column - shift).astype(
        jnp.float32
    )
    picked = jnp.dot(
        potential,
        select.reshape(col_count, half_count * local_cols),
        precision=lax.Precision.HIGHEST,
    )
    return COUPLING * picked.reshape(potential.shape[0], half_count, local_cols)


def lookup(region, values_table):
    classes = jnp.arange(values_table.shape[0], dtype=jnp.int32)
    return jnp.sum(jnp.where(region[..., None] == classes, values_table, 0.0), axis=-1)


def xor_pairs(count, bit):
    return [(i, i ^ bit) for i in range(count)]


def sum_over(value, axis):
    count = lax.axis_size(axis)
    bit = 1
    while bit < count:
        value = value + lax.ppermute(value, axis, xor_pairs(count, bit))
        bit *= 2
    return value


def gather_rows(value, axis, bits):
    count = lax.axis_size(axis)
    index = lax.axis_index(axis)
    for bit in bits:
        other = lax.ppermute(value, axis, xor_pairs(count, bit))
        low = (index & bit) == 0
        value = jnp.where(
            low, jnp.concatenate([value, other], 0), jnp.concatenate([other, value], 0)
        )
    return value


def in_row_order(value, bits, count):
    levels = len(bits)
    shaped = value.reshape((2,) * levels + (-1,) + value.shape[1:])
    order = sorted(range(levels), key=lambda axis: -bits[levels - 1 - axis])
    shaped = jnp.transpose(shaped, order + list(range(levels, shaped.ndim)))
    return shaped.reshape((count,) + value.shape[1:])


def shards(distribution, region, region_doping, region_relax, equilibrium, kx_speed, upwind_sign):
    precise = lax.Precision.HIGHEST
    triple = lax.Precision.HIGH
    row_count, ky_local, col_count, kx_count = distribution.shape
    ky_count = ky_local * lax.axis_size("ky")
    space_count = lax.axis_size("space")
    grid_rows = row_count * space_count
    space_index = lax.axis_index("space")
    row_start = space_index * row_count

    partial_value = jnp.sum(distribution, axis=(1, 3)) / (ky_count * kx_count)
    density = sum_over(partial_value, "ky")
    doping = lookup(region, region_doping)
    relax_rate = lookup(region, region_relax)
    charge = density - doping
    far_bits = [bit for bit in (8, 16, 32) if bit < space_count]
    near_bits = [bit for bit in (1, 2, 4) if bit < space_count]
    positive_kx = upwind_sign > 0
    half_kx = kx_count // 2
    rank_pos = jnp.cumsum(positive_kx.astype(jnp.int32)) - 1
    rank_neg = jnp.cumsum((~positive_kx).astype(jnp.int32)) - 1
    slots = jnp.arange(half_kx, dtype=jnp.int32)
    pick_pos = (positive_kx[:, None] & (rank_pos[:, None] == slots[None, :])).astype(jnp.float32)
    pick_neg = ((~positive_kx)[:, None] & (rank_neg[:, None] == slots[None, :])).astype(jnp.float32)
    flat = distribution.reshape(-1, kx_count)
    send_right = jnp.dot(flat, pick_pos, precision=precise)
    send_left = jnp.dot(flat, pick_neg, precision=precise)
    forward_pairs = [(i, i + 1) for i in range(space_count - 1)]
    backward_pairs = [(i + 1, i) for i in range(space_count - 1)]
    got_left = lax.ppermute(send_right, "space", forward_pairs)
    got_right = lax.ppermute(send_left, "space", backward_pairs)
    far_rows = gather_rows(charge, "space", far_bits)
    held, far_rows, got_left, got_right = lax.optimization_barrier(
        (distribution, far_rows, got_left, got_right)
    )
    every_row = gather_rows(far_rows, "space", near_bits)
    every_row = in_row_order(every_row, far_bits + near_bits, space_count * row_count)

    sine_rows = sine_table(grid_rows)
    sine_cols = sine_table(col_count)
    eigen_cols = eigen_values(col_count)
    along_x = jnp.dot(sine_rows, every_row, precision=precise)
    spectral = jnp.dot(along_x, sine_cols, precision=precise)
    spectral = spectral / (eigen_values(grid_rows)[:, None] + eigen_cols[None, :])
    back_cols = jnp.dot(spectral, sine_cols, precision=precise)
    own_rows = lax.dynamic_slice_in_dim(sine_rows, row_start, row_count, 0)
    potential = POISSON * jnp.dot(own_rows, back_cols, precision=precise)

    spread = lax.all_to_all(held, "ky", split_axis=2, concat_axis=1, tiled=True)
    local_cols = spread.shape[2]
    forward, backward = wigner_tables(ky_count)
    weights = own_differences(potential, ky_count, lax.axis_index("ky") * local_cols, local_cols)
    flattened = spread.reshape(row_count, ky_count, local_cols * kx_count)
    coeffs = jnp.einsum("ab,rbm->ram", forward, flattened, precision=triple)
    coeffs = coeffs.reshape(row_count, ky_count, local_cols, kx_count)
    scaled = coeffs * jnp.concatenate([weights, weights], axis=1)[..., None]
    mixed = jnp.einsum(
        "ab,rbm->ram",
        backward,
        scaled.reshape(row_count, ky_count, local_cols * kx_count),
        precision=triple,
    )
    mixed = mixed.reshape(row_count, ky_count, local_cols, kx_count)
    wigner = lax.all_to_all(mixed, "ky", split_axis=1, concat_axis=2, tiled=True)

    upstream_x = jnp.dot(got_left, pick_pos.T, precision=precise) + jnp.dot(
        got_right, pick_neg.T, precision=precise
    )
    upstream_x = upstream_x.reshape(distribution.shape)
    drift_x = -kx_speed[None, None, None, :] * (distribution - upstream_x)

    ky_global = lax.axis_index("ky") * ky_local + jnp.arange(ky_local, dtype=jnp.int32)
    upward = ky_global >= ky_count // 2
    vertical = DRIFT_Y * (ky_global.astype(jnp.float32) + 0.5 - 0.5 * ky_count) / (0.5 * ky_count)
    zero_col = jnp.zeros_like(distribution[:, :, :1])
    from_low = jnp.concatenate([zero_col, distribution[:, :, :-1]], axis=2)
    from_high = jnp.concatenate([distribution[:, :, 1:], zero_col], axis=2)
    upstream_y = jnp.where(upward[None, :, None, None], from_low, from_high)
    drift_y = -jnp.abs(vertical)[None, :, None, None] * (distribution - upstream_y)
    relaxation = relax_rate[:, None, :, None] * (
        density[:, None, :, None] * equilibrium[None, :, None, :] - distribution
    )
    return distribution + STEP * (drift_x + drift_y + wigner + relaxation)


def solution(mesh):
    return jax.shard_map(
        shards,
        mesh=mesh,
        in_specs=(
            P("space", "ky", None, None),
            P("space", None),
            P(),
            P(),
            P("ky", None),
            P(),
            P(),
        ),
        out_specs=P("space", "ky", None, None),
        check_vma=False,
    )
```

```python
import math

import jax
import jax.numpy as jnp
from jax import lax
from jax.sharding import PartitionSpec as P

COUPLING = 0.04
POISSON = 0.1
STEP = 0.4
DRIFT_Y = 0.8


def sine_table(length):
    positions = jnp.arange(1, length + 1, dtype=jnp.int32)
    phase_index = positions[:, None] * positions[None, :] % (2 * length + 2)
    return jnp.sqrt(2.0 / (length + 1.0)) * jnp.sin(
        math.pi * phase_index.astype(jnp.float32) / (length + 1.0)
    )


def eigen_values(length):
    positions = jnp.arange(1, length + 1, dtype=jnp.int32).astype(jnp.float32)
    return 4.0 * jnp.sin(0.5 * math.pi * positions / (length + 1.0)) ** 2


def wigner_tables(modes):
    half_count = modes // 2
    shifts = jnp.arange(1, half_count + 1, dtype=jnp.int32)
    wave_index = jnp.arange(modes, dtype=jnp.int32)
    phase_index = shifts[:, None] * wave_index[None, :] % modes
    angles = 2.0 * math.pi / modes * phase_index.astype(jnp.float32)
    forward = jnp.concatenate([jnp.cos(angles), jnp.sin(angles)], axis=0)
    backward = jnp.concatenate([jnp.sin(angles).T, -jnp.cos(angles).T], axis=1)
    return (forward, backward)


def own_differences(potential, modes, first_col, local_cols):
    half_count = modes // 2
    col_count = potential.shape[1]
    source = jnp.arange(col_count, dtype=jnp.int32)[:, None, None]
    shift = jnp.arange(1, half_count + 1, dtype=jnp.int32)[None, :, None]
    column = first_col + jnp.arange(local_cols, dtype=jnp.int32)[None, None, :]
    select = (source == column + shift).astype(jnp.float32) - (source == column - shift).astype(
        jnp.float32
    )
    picked = jnp.dot(
        potential,
        select.reshape(col_count, half_count * local_cols),
        precision=lax.Precision.HIGHEST,
    )
    return COUPLING * picked.reshape(potential.shape[0], half_count, local_cols)


def lookup(region, values_table):
    classes = jnp.arange(values_table.shape[0], dtype=jnp.int32)
    return jnp.sum(jnp.where(region[..., None] == classes, values_table, 0.0), axis=-1)


def xor_pairs(count, bit):
    return [(i, i ^ bit) for i in range(count)]


def sum_over(value, axis):
    count = lax.axis_size(axis)
    bit = 1
    while bit < count:
        value = value + lax.ppermute(value, axis, xor_pairs(count, bit))
        bit *= 2
    return value


def gather_rows(value, axis, bits):
    count = lax.axis_size(axis)
    index = lax.axis_index(axis)
    for bit in bits:
        other = lax.ppermute(value, axis, xor_pairs(count, bit))
        low = (index & bit) == 0
        value = jnp.where(
            low, jnp.concatenate([value, other], 0), jnp.concatenate([other, value], 0)
        )
    return value


def in_row_order(value, bits, count):
    levels = len(bits)
    shaped = value.reshape((2,) * levels + (-1,) + value.shape[1:])
    order = sorted(range(levels), key=lambda axis: -bits[levels - 1 - axis])
    shaped = jnp.transpose(shaped, order + list(range(levels, shaped.ndim)))
    return shaped.reshape((count,) + value.shape[1:])


def shards(distribution, region, region_doping, region_relax, equilibrium, kx_speed, upwind_sign):
    precise = lax.Precision.HIGHEST
    triple = lax.Precision.HIGH
    row_count, ky_local, col_count, kx_count = distribution.shape
    ky_count = ky_local * lax.axis_size("ky")
    space_count = lax.axis_size("space")
    grid_rows = row_count * space_count
    space_index = lax.axis_index("space")
    row_start = space_index * row_count

    partial_value = jnp.sum(distribution, axis=(1, 3)) / (ky_count * kx_count)
    density = sum_over(partial_value, "ky")
    doping = lookup(region, region_doping)
    relax_rate = lookup(region, region_relax)
    charge = density - doping
    far_bits = [bit for bit in (8, 16, 32) if bit < space_count]
    near_bits = [bit for bit in (1, 2, 4) if bit < space_count]
    positive_kx = upwind_sign > 0
    half_kx = kx_count // 2
    rank_pos = jnp.cumsum(positive_kx.astype(jnp.int32)) - 1
    rank_neg = jnp.cumsum((~positive_kx).astype(jnp.int32)) - 1
    slots = jnp.arange(half_kx, dtype=jnp.int32)
    pick_pos = (positive_kx[:, None] & (rank_pos[:, None] == slots[None, :])).astype(jnp.float32)
    pick_neg = ((~positive_kx)[:, None] & (rank_neg[:, None] == slots[None, :])).astype(jnp.float32)
    flat = distribution.reshape(-1, kx_count)
    send_right = jnp.dot(flat, pick_pos, precision=precise)
    send_left = jnp.dot(flat, pick_neg, precision=precise)
    forward_pairs = [(i, i + 1) for i in range(space_count - 1)]
    backward_pairs = [(i + 1, i) for i in range(space_count - 1)]
    got_left = lax.ppermute(send_right, "space", forward_pairs)
    got_right = lax.ppermute(send_left, "space", backward_pairs)
    far_rows = gather_rows(charge, "space", far_bits)
    every_row = gather_rows(far_rows, "space", near_bits)
    every_row = in_row_order(every_row, far_bits + near_bits, space_count * row_count)

    sine_rows = sine_table(grid_rows)
    sine_cols = sine_table(col_count)
    eigen_cols = eigen_values(col_count)
    along_x = jnp.dot(sine_rows, every_row, precision=precise)
    spectral = jnp.dot(along_x, sine_cols, precision=precise)
    spectral = spectral / (eigen_values(grid_rows)[:, None] + eigen_cols[None, :])
    back_cols = jnp.dot(spectral, sine_cols, precision=precise)
    own_rows = lax.dynamic_slice_in_dim(sine_rows, row_start, row_count, 0)
    potential = POISSON * jnp.dot(own_rows, back_cols, precision=precise)

    spread = lax.all_to_all(distribution, "ky", split_axis=2, concat_axis=1, tiled=True)
    local_cols = spread.shape[2]
    forward, backward = wigner_tables(ky_count)
    weights = own_differences(potential, ky_count, lax.axis_index("ky") * local_cols, local_cols)
    flattened = spread.reshape(row_count, ky_count, local_cols * kx_count)
    coeffs = jnp.einsum("ab,rbm->ram", forward, flattened, precision=triple)
    coeffs = coeffs.reshape(row_count, ky_count, local_cols, kx_count)
    scaled = coeffs * jnp.concatenate([weights, weights], axis=1)[..., None]
    mixed = jnp.einsum(
        "ab,rbm->ram",
        backward,
        scaled.reshape(row_count, ky_count, local_cols * kx_count),
        precision=triple,
    )
    mixed = mixed.reshape(row_count, ky_count, local_cols, kx_count)
    mixed, got_left, got_right = lax.optimization_barrier((mixed, got_left, got_right))
    wigner = lax.all_to_all(mixed, "ky", split_axis=1, concat_axis=2, tiled=True)

    upstream_x = jnp.dot(got_left, pick_pos.T, precision=precise) + jnp.dot(
        got_right, pick_neg.T, precision=precise
    )
    upstream_x = upstream_x.reshape(distribution.shape)
    drift_x = -kx_speed[None, None, None, :] * (distribution - upstream_x)

    ky_global = lax.axis_index("ky") * ky_local + jnp.arange(ky_local, dtype=jnp.int32)
    upward = ky_global >= ky_count // 2
    vertical = DRIFT_Y * (ky_global.astype(jnp.float32) + 0.5 - 0.5 * ky_count) / (0.5 * ky_count)
    zero_col = jnp.zeros_like(distribution[:, :, :1])
    from_low = jnp.concatenate([zero_col, distribution[:, :, :-1]], axis=2)
    from_high = jnp.concatenate([distribution[:, :, 1:], zero_col], axis=2)
    upstream_y = jnp.where(upward[None, :, None, None], from_low, from_high)
    drift_y = -jnp.abs(vertical)[None, :, None, None] * (distribution - upstream_y)
    relaxation = relax_rate[:, None, :, None] * (
        density[:, None, :, None] * equilibrium[None, :, None, :] - distribution
    )
    return distribution + STEP * (drift_x + drift_y + wigner + relaxation)


def solution(mesh):
    return jax.shard_map(
        shards,
        mesh=mesh,
        in_specs=(
            P("space", "ky", None, None),
            P("space", None),
            P(),
            P(),
            P("ky", None),
            P(),
            P(),
        ),
        out_specs=P("space", "ky", None, None),
        check_vma=False,
    )
```

```python
import math

import jax
import jax.numpy as jnp
from jax import lax
from jax.sharding import PartitionSpec as P

COUPLING = 0.04
POISSON = 0.1
STEP = 0.4
DRIFT_Y = 0.8


def sine_table(length):
    positions = jnp.arange(1, length + 1, dtype=jnp.int32)
    phase_index = positions[:, None] * positions[None, :] % (2 * length + 2)
    return jnp.sqrt(2.0 / (length + 1.0)) * jnp.sin(
        math.pi * phase_index.astype(jnp.float32) / (length + 1.0)
    )


def eigen_values(length):
    positions = jnp.arange(1, length + 1, dtype=jnp.int32).astype(jnp.float32)
    return 4.0 * jnp.sin(0.5 * math.pi * positions / (length + 1.0)) ** 2


def wigner_tables(modes):
    half_count = modes // 2
    shifts = jnp.arange(1, half_count + 1, dtype=jnp.int32)
    wave_index = jnp.arange(modes, dtype=jnp.int32)
    phase_index = shifts[:, None] * wave_index[None, :] % modes
    angles = 2.0 * math.pi / modes * phase_index.astype(jnp.float32)
    forward = jnp.concatenate([jnp.cos(angles), jnp.sin(angles)], axis=0)
    backward = jnp.concatenate([jnp.sin(angles).T, -jnp.cos(angles).T], axis=1)
    return (forward, backward)


def own_differences(potential, modes, first_col, local_cols):
    half_count = modes // 2
    col_count = potential.shape[1]
    source = jnp.arange(col_count, dtype=jnp.int32)[:, None, None]
    shift = jnp.arange(1, half_count + 1, dtype=jnp.int32)[None, :, None]
    column = first_col + jnp.arange(local_cols, dtype=jnp.int32)[None, None, :]
    select = (source == column + shift).astype(jnp.float32) - (source == column - shift).astype(
        jnp.float32
    )
    picked = jnp.dot(
        potential,
        select.reshape(col_count, half_count * local_cols),
        precision=lax.Precision.HIGHEST,
    )
    return COUPLING * picked.reshape(potential.shape[0], half_count, local_cols)


def lookup(region, values_table):
    classes = jnp.arange(values_table.shape[0], dtype=jnp.int32)
    return jnp.sum(jnp.where(region[..., None] == classes, values_table, 0.0), axis=-1)


def xor_pairs(count, bit):
    return [(i, i ^ bit) for i in range(count)]


def sum_over(value, axis, bits):
    count = lax.axis_size(axis)
    for bit in bits:
        value = value + lax.ppermute(value, axis, xor_pairs(count, bit))
    return value


def gather_rows(value, axis, bits):
    count = lax.axis_size(axis)
    index = lax.axis_index(axis)
    for bit in bits:
        other = lax.ppermute(value, axis, xor_pairs(count, bit))
        low = (index & bit) == 0
        value = jnp.where(
            low, jnp.concatenate([value, other], 0), jnp.concatenate([other, value], 0)
        )
    return value


def in_row_order(value, bits, count):
    levels = len(bits)
    shaped = value.reshape((2,) * levels + (-1,) + value.shape[1:])
    order = sorted(range(levels), key=lambda axis: -bits[levels - 1 - axis])
    shaped = jnp.transpose(shaped, order + list(range(levels, shaped.ndim)))
    return shaped.reshape((count,) + value.shape[1:])


def shards(distribution, region, region_doping, region_relax, equilibrium, kx_speed, upwind_sign):
    precise = lax.Precision.HIGHEST
    triple = lax.Precision.HIGH
    row_count, ky_local, col_count, kx_count = distribution.shape
    ky_count = ky_local * lax.axis_size("ky")
    space_count = lax.axis_size("space")
    grid_rows = row_count * space_count
    space_index = lax.axis_index("space")
    row_start = space_index * row_count

    partial_value = jnp.sum(distribution, axis=(1, 3)) / (ky_count * kx_count)
    doping = lookup(region, region_doping)
    relax_rate = lookup(region, region_relax)
    ky_size = lax.axis_size("ky")
    z_bits = [ky_size // 2] if ky_size > 1 else []
    y_bits = [bit for bit in (1, 2, 4, 8, 16) if bit < ky_size // 2]
    partial_charge = partial_value - jnp.where(lax.axis_index("ky") == 0, doping, 0.0)
    charge = sum_over(jnp.stack([partial_value, partial_charge], axis=1), "ky", z_bits)
    far_bits = [bit for bit in (8, 16, 32) if bit < space_count]
    near_bits = [bit for bit in (1, 2, 4) if bit < space_count]
    positive_kx = upwind_sign > 0
    half_kx = kx_count // 2
    rank_pos = jnp.cumsum(positive_kx.astype(jnp.int32)) - 1
    rank_neg = jnp.cumsum((~positive_kx).astype(jnp.int32)) - 1
    slots = jnp.arange(half_kx, dtype=jnp.int32)
    pick_pos = (positive_kx[:, None] & (rank_pos[:, None] == slots[None, :])).astype(jnp.float32)
    pick_neg = ((~positive_kx)[:, None] & (rank_neg[:, None] == slots[None, :])).astype(jnp.float32)
    flat = distribution.reshape(-1, kx_count)
    send_right = jnp.dot(flat, pick_pos, precision=precise)
    send_left = jnp.dot(flat, pick_neg, precision=precise)
    forward_pairs = [(i, i + 1) for i in range(space_count - 1)]
    backward_pairs = [(i + 1, i) for i in range(space_count - 1)]
    got_left = lax.ppermute(send_right, "space", forward_pairs)
    got_right = lax.ppermute(send_left, "space", backward_pairs)
    far_rows = gather_rows(charge, "space", far_bits)
    held, far_rows, got_left, got_right = lax.optimization_barrier(
        (distribution, far_rows, got_left, got_right)
    )
    every_row = gather_rows(far_rows, "space", near_bits)
    every_row = in_row_order(every_row, far_bits + near_bits, space_count * row_count)
    every_row = sum_over(every_row, "ky", y_bits)
    density = lax.dynamic_slice_in_dim(every_row[:, 0], row_start, row_count, 0)
    every_row = every_row[:, 1]

    sine_rows = sine_table(grid_rows)
    sine_cols = sine_table(col_count)
    eigen_cols = eigen_values(col_count)
    along_x = jnp.dot(sine_rows, every_row, precision=precise)
    spectral = jnp.dot(along_x, sine_cols, precision=precise)
    spectral = spectral / (eigen_values(grid_rows)[:, None] + eigen_cols[None, :])
    back_cols = jnp.dot(spectral, sine_cols, precision=precise)
    own_rows = lax.dynamic_slice_in_dim(sine_rows, row_start, row_count, 0)
    potential = POISSON * jnp.dot(own_rows, back_cols, precision=precise)

    spread = lax.all_to_all(held, "ky", split_axis=2, concat_axis=1, tiled=True)
    local_cols = spread.shape[2]
    forward, backward = wigner_tables(ky_count)
    weights = own_differences(potential, ky_count, lax.axis_index("ky") * local_cols, local_cols)
    flattened = spread.reshape(row_count, ky_count, local_cols * kx_count)
    coeffs = jnp.einsum("ab,rbm->ram", forward, flattened, precision=triple)
    coeffs = coeffs.reshape(row_count, ky_count, local_cols, kx_count)
    scaled = coeffs * jnp.concatenate([weights, weights], axis=1)[..., None]
    mixed = jnp.einsum(
        "ab,rbm->ram",
        backward,
        scaled.reshape(row_count, ky_count, local_cols * kx_count),
        precision=triple,
    )
    mixed = mixed.reshape(row_count, ky_count, local_cols, kx_count)
    wigner = lax.all_to_all(mixed, "ky", split_axis=1, concat_axis=2, tiled=True)

    upstream_x = jnp.dot(got_left, pick_pos.T, precision=precise) + jnp.dot(
        got_right, pick_neg.T, precision=precise
    )
    upstream_x = upstream_x.reshape(distribution.shape)
    drift_x = -kx_speed[None, None, None, :] * (distribution - upstream_x)

    ky_global = lax.axis_index("ky") * ky_local + jnp.arange(ky_local, dtype=jnp.int32)
    upward = ky_global >= ky_count // 2
    vertical = DRIFT_Y * (ky_global.astype(jnp.float32) + 0.5 - 0.5 * ky_count) / (0.5 * ky_count)
    zero_col = jnp.zeros_like(distribution[:, :, :1])
    from_low = jnp.concatenate([zero_col, distribution[:, :, :-1]], axis=2)
    from_high = jnp.concatenate([distribution[:, :, 1:], zero_col], axis=2)
    upstream_y = jnp.where(upward[None, :, None, None], from_low, from_high)
    drift_y = -jnp.abs(vertical)[None, :, None, None] * (distribution - upstream_y)
    relaxation = relax_rate[:, None, :, None] * (
        density[:, None, :, None] * equilibrium[None, :, None, :] - distribution
    )
    return distribution + STEP * (drift_x + drift_y + wigner + relaxation)


def solution(mesh):
    return jax.shard_map(
        shards,
        mesh=mesh,
        in_specs=(
            P("space", "ky", None, None),
            P("space", None),
            P(),
            P(),
            P("ky", None),
            P(),
            P(),
        ),
        out_specs=P("space", "ky", None, None),
        check_vma=False,
    )
```

```python
import math

import jax
import jax.numpy as jnp
from jax import lax
from jax.sharding import PartitionSpec as P

COUPLING = 0.04
POISSON = 0.1
STEP = 0.4
DRIFT_Y = 0.8


def sine_table(length):
    positions = jnp.arange(1, length + 1, dtype=jnp.int32)
    phase_index = positions[:, None] * positions[None, :] % (2 * length + 2)
    return jnp.sqrt(2.0 / (length + 1.0)) * jnp.sin(
        math.pi * phase_index.astype(jnp.float32) / (length + 1.0)
    )


def eigen_values(length):
    positions = jnp.arange(1, length + 1, dtype=jnp.int32).astype(jnp.float32)
    return 4.0 * jnp.sin(0.5 * math.pi * positions / (length + 1.0)) ** 2


def wigner_tables(modes):
    half_count = modes // 2
    shifts = jnp.arange(1, half_count + 1, dtype=jnp.int32)
    wave_index = jnp.arange(modes, dtype=jnp.int32)
    phase_index = shifts[:, None] * wave_index[None, :] % modes
    angles = 2.0 * math.pi / modes * phase_index.astype(jnp.float32)
    forward = jnp.concatenate([jnp.cos(angles), jnp.sin(angles)], axis=0)
    backward = jnp.concatenate([jnp.sin(angles).T, -jnp.cos(angles).T], axis=1)
    return (forward, backward)


def own_differences(potential, modes, first_col, local_cols):
    half_count = modes // 2
    col_count = potential.shape[1]
    source = jnp.arange(col_count, dtype=jnp.int32)[:, None, None]
    shift = jnp.arange(1, half_count + 1, dtype=jnp.int32)[None, :, None]
    column = first_col + jnp.arange(local_cols, dtype=jnp.int32)[None, None, :]
    select = (source == column + shift).astype(jnp.float32) - (source == column - shift).astype(
        jnp.float32
    )
    picked = jnp.dot(
        potential,
        select.reshape(col_count, half_count * local_cols),
        precision=lax.Precision.HIGHEST,
    )
    return COUPLING * picked.reshape(potential.shape[0], half_count, local_cols)


def lookup(region, values_table):
    classes = jnp.arange(values_table.shape[0], dtype=jnp.int32)
    return jnp.sum(jnp.where(region[..., None] == classes, values_table, 0.0), axis=-1)


def xor_pairs(count, bit):
    return [(i, i ^ bit) for i in range(count)]


def sum_over(value, axis, bits):
    count = lax.axis_size(axis)
    for bit in bits:
        value = value + lax.ppermute(value, axis, xor_pairs(count, bit))
    return value


def gather_rows(value, axis, bits):
    count = lax.axis_size(axis)
    index = lax.axis_index(axis)
    for bit in bits:
        other = lax.ppermute(value, axis, xor_pairs(count, bit))
        low = (index & bit) == 0
        value = jnp.where(
            low, jnp.concatenate([value, other], 0), jnp.concatenate([other, value], 0)
        )
    return value


def in_row_order(value, bits, count):
    levels = len(bits)
    shaped = value.reshape((2,) * levels + (-1,) + value.shape[1:])
    order = sorted(range(levels), key=lambda axis: -bits[levels - 1 - axis])
    shaped = jnp.transpose(shaped, order + list(range(levels, shaped.ndim)))
    return shaped.reshape((count,) + value.shape[1:])


def spread_columns(block, first):
    ky_size = lax.axis_size("ky")
    quad = ky_size // 2
    index = lax.axis_index("ky")
    half, place = index // quad, index % quad
    rows, ky_local, col_count, kx_count = block.shape
    width = col_count // ky_size
    blocks = block.reshape(rows, ky_local, 2, quad, width, kx_count)
    received = []
    for shift in range(quad):
        piece = lax.dynamic_index_in_dim(blocks, (place + shift) % quad, 3, keepdims=False)
        if shift:
            pairs = [(h * quad + i, h * quad + (i + shift) % quad) for h in range(2) for i in range(quad)]
            piece = lax.ppermute(piece, "ky", pairs)
        received.append(piece)
    stacked = jnp.stack(received, 0)
    stacked = jnp.take(stacked, (place - jnp.arange(quad)) % quad, axis=0)
    stacked = jnp.moveaxis(stacked, 3, 0)
    stacked = lax.optimization_barrier((stacked, first))[0]
    keep = lax.dynamic_index_in_dim(stacked, half, 0, keepdims=False)
    send = lax.dynamic_index_in_dim(stacked, 1 - half, 0, keepdims=False)
    got = lax.ppermute(send, "ky", [(i, i ^ quad) for i in range(ky_size)])
    low = jnp.where(half == 0, keep, got)
    high = jnp.where(half == 0, got, keep)
    whole = jnp.concatenate([low, high], 0)
    whole = jnp.moveaxis(whole, 1, 0)
    return whole.reshape(rows, 2 * quad * ky_local, width, kx_count)


def shards(distribution, region, region_doping, region_relax, equilibrium, kx_speed, upwind_sign):
    precise = lax.Precision.HIGHEST
    triple = lax.Precision.HIGH
    row_count, ky_local, col_count, kx_count = distribution.shape
    ky_count = ky_local * lax.axis_size("ky")
    space_count = lax.axis_size("space")
    grid_rows = row_count * space_count
    space_index = lax.axis_index("space")
    row_start = space_index * row_count

    partial_value = jnp.sum(distribution, axis=(1, 3)) / (ky_count * kx_count)
    doping = lookup(region, region_doping)
    relax_rate = lookup(region, region_relax)
    ky_size = lax.axis_size("ky")
    z_bits = [ky_size // 2] if ky_size > 1 else []
    y_bits = [bit for bit in (1, 2, 4, 8, 16) if bit < ky_size // 2]
    partial_charge = partial_value - jnp.where(lax.axis_index("ky") == 0, doping, 0.0)
    charge = sum_over(jnp.stack([partial_value, partial_charge], axis=1), "ky", z_bits)
    far_bits = [bit for bit in (8, 16, 32) if bit < space_count]
    near_bits = [bit for bit in (1, 2, 4) if bit < space_count]
    positive_kx = upwind_sign > 0
    half_kx = kx_count // 2
    rank_pos = jnp.cumsum(positive_kx.astype(jnp.int32)) - 1
    rank_neg = jnp.cumsum((~positive_kx).astype(jnp.int32)) - 1
    slots = jnp.arange(half_kx, dtype=jnp.int32)
    pick_pos = (positive_kx[:, None] & (rank_pos[:, None] == slots[None, :])).astype(jnp.float32)
    pick_neg = ((~positive_kx)[:, None] & (rank_neg[:, None] == slots[None, :])).astype(jnp.float32)
    flat = distribution.reshape(-1, kx_count)
    send_right = jnp.dot(flat, pick_pos, precision=precise)
    send_left = jnp.dot(flat, pick_neg, precision=precise)
    forward_pairs = [(i, i + 1) for i in range(space_count - 1)]
    backward_pairs = [(i + 1, i) for i in range(space_count - 1)]
    got_left = lax.ppermute(send_right, "space", forward_pairs)
    got_right = lax.ppermute(send_left, "space", backward_pairs)
    far_rows = gather_rows(charge, "space", far_bits)
    far_rows, got_left, got_right = lax.optimization_barrier((far_rows, got_left, got_right))
    every_row = gather_rows(far_rows, "space", near_bits)
    every_row = in_row_order(every_row, far_bits + near_bits, space_count * row_count)
    every_row = sum_over(every_row, "ky", y_bits)
    density = lax.dynamic_slice_in_dim(every_row[:, 0], row_start, row_count, 0)
    every_row = every_row[:, 1]

    sine_rows = sine_table(grid_rows)
    sine_cols = sine_table(col_count)
    eigen_cols = eigen_values(col_count)
    along_x = jnp.dot(sine_rows, every_row, precision=precise)
    spectral = jnp.dot(along_x, sine_cols, precision=precise)
    spectral = spectral / (eigen_values(grid_rows)[:, None] + eigen_cols[None, :])
    back_cols = jnp.dot(spectral, sine_cols, precision=precise)
    own_rows = lax.dynamic_slice_in_dim(sine_rows, row_start, row_count, 0)
    potential = POISSON * jnp.dot(own_rows, back_cols, precision=precise)

    spread = spread_columns(distribution, far_rows)
    local_cols = spread.shape[2]
    forward, backward = wigner_tables(ky_count)
    weights = own_differences(potential, ky_count, lax.axis_index("ky") * local_cols, local_cols)
    flattened = spread.reshape(row_count, ky_count, local_cols * kx_count)
    coeffs = jnp.einsum("ab,rbm->ram", forward, flattened, precision=triple)
    coeffs = coeffs.reshape(row_count, ky_count, local_cols, kx_count)
    scaled = coeffs * jnp.concatenate([weights, weights], axis=1)[..., None]
    mixed = jnp.einsum(
        "ab,rbm->ram",
        backward,
        scaled.reshape(row_count, ky_count, local_cols * kx_count),
        precision=triple,
    )
    mixed = mixed.reshape(row_count, ky_count, local_cols, kx_count)
    wigner = lax.all_to_all(mixed, "ky", split_axis=1, concat_axis=2, tiled=True)

    upstream_x = jnp.dot(got_left, pick_pos.T, precision=precise) + jnp.dot(
        got_right, pick_neg.T, precision=precise
    )
    upstream_x = upstream_x.reshape(distribution.shape)
    drift_x = -kx_speed[None, None, None, :] * (distribution - upstream_x)

    ky_global = lax.axis_index("ky") * ky_local + jnp.arange(ky_local, dtype=jnp.int32)
    upward = ky_global >= ky_count // 2
    vertical = DRIFT_Y * (ky_global.astype(jnp.float32) + 0.5 - 0.5 * ky_count) / (0.5 * ky_count)
    zero_col = jnp.zeros_like(distribution[:, :, :1])
    from_low = jnp.concatenate([zero_col, distribution[:, :, :-1]], axis=2)
    from_high = jnp.concatenate([distribution[:, :, 1:], zero_col], axis=2)
    upstream_y = jnp.where(upward[None, :, None, None], from_low, from_high)
    drift_y = -jnp.abs(vertical)[None, :, None, None] * (distribution - upstream_y)
    relaxation = relax_rate[:, None, :, None] * (
        density[:, None, :, None] * equilibrium[None, :, None, :] - distribution
    )
    return distribution + STEP * (drift_x + drift_y + wigner + relaxation)


def solution(mesh):
    return jax.shard_map(
        shards,
        mesh=mesh,
        in_specs=(
            P("space", "ky", None, None),
            P("space", None),
            P(),
            P(),
            P("ky", None),
            P(),
            P(),
        ),
        out_specs=P("space", "ky", None, None),
        check_vma=False,
    )
```

```python
import math

import jax
import jax.numpy as jnp
from jax import lax
from jax.sharding import PartitionSpec as P

COUPLING = 0.04
POISSON = 0.1
STEP = 0.4
DRIFT_Y = 0.8


def sine_table(length):
    positions = jnp.arange(1, length + 1, dtype=jnp.int32)
    phase_index = positions[:, None] * positions[None, :] % (2 * length + 2)
    return jnp.sqrt(2.0 / (length + 1.0)) * jnp.sin(
        math.pi * phase_index.astype(jnp.float32) / (length + 1.0)
    )


def eigen_values(length):
    positions = jnp.arange(1, length + 1, dtype=jnp.int32).astype(jnp.float32)
    return 4.0 * jnp.sin(0.5 * math.pi * positions / (length + 1.0)) ** 2


def wigner_tables(modes):
    half_count = modes // 2
    shifts = jnp.arange(1, half_count + 1, dtype=jnp.int32)
    wave_index = jnp.arange(modes, dtype=jnp.int32)
    phase_index = shifts[:, None] * wave_index[None, :] % modes
    angles = 2.0 * math.pi / modes * phase_index.astype(jnp.float32)
    forward = jnp.concatenate([jnp.cos(angles), jnp.sin(angles)], axis=0)
    backward = jnp.concatenate([jnp.sin(angles).T, -jnp.cos(angles).T], axis=1)
    return (forward, backward)


def own_differences(potential, modes, first_col, local_cols):
    half_count = modes // 2
    col_count = potential.shape[1]
    source = jnp.arange(col_count, dtype=jnp.int32)[:, None, None]
    shift = jnp.arange(1, half_count + 1, dtype=jnp.int32)[None, :, None]
    column = first_col + jnp.arange(local_cols, dtype=jnp.int32)[None, None, :]
    select = (source == column + shift).astype(jnp.float32) - (source == column - shift).astype(
        jnp.float32
    )
    picked = jnp.dot(
        potential,
        select.reshape(col_count, half_count * local_cols),
        precision=lax.Precision.HIGHEST,
    )
    return COUPLING * picked.reshape(potential.shape[0], half_count, local_cols)


def lookup(region, values_table):
    classes = jnp.arange(values_table.shape[0], dtype=jnp.int32)
    return jnp.sum(jnp.where(region[..., None] == classes, values_table, 0.0), axis=-1)


def xor_pairs(count, bit):
    return [(i, i ^ bit) for i in range(count)]


def sum_over(value, axis, bits):
    count = lax.axis_size(axis)
    for bit in bits:
        value = value + lax.ppermute(value, axis, xor_pairs(count, bit))
    return value


def gather_rows(value, axis, bits):
    count = lax.axis_size(axis)
    index = lax.axis_index(axis)
    for bit in bits:
        other = lax.ppermute(value, axis, xor_pairs(count, bit))
        low = (index & bit) == 0
        value = jnp.where(
            low, jnp.concatenate([value, other], 0), jnp.concatenate([other, value], 0)
        )
    return value


def in_row_order(value, bits, count):
    levels = len(bits)
    shaped = value.reshape((2,) * levels + (-1,) + value.shape[1:])
    order = sorted(range(levels), key=lambda axis: -bits[levels - 1 - axis])
    shaped = jnp.transpose(shaped, order + list(range(levels, shaped.ndim)))
    return shaped.reshape((count,) + value.shape[1:])


def shards(distribution, region, region_doping, region_relax, equilibrium, kx_speed, upwind_sign):
    precise = lax.Precision.HIGHEST
    triple = lax.Precision.HIGH
    row_count, ky_local, col_count, kx_count = distribution.shape
    ky_count = ky_local * lax.axis_size("ky")
    space_count = lax.axis_size("space")
    grid_rows = row_count * space_count
    space_index = lax.axis_index("space")
    row_start = space_index * row_count

    partial_value = jnp.sum(distribution, axis=(1, 3)) / (ky_count * kx_count)
    doping = lookup(region, region_doping)
    relax_rate = lookup(region, region_relax)
    ky_size = lax.axis_size("ky")
    z_bits = [ky_size // 2] if ky_size > 1 else []
    y_bits = [bit for bit in (1, 2, 4, 8, 16) if bit < ky_size // 2]
    partial_charge = partial_value - jnp.where(lax.axis_index("ky") == 0, doping, 0.0)
    charge = sum_over(jnp.stack([partial_value, partial_charge], axis=1), "ky", z_bits)
    far_bits = [bit for bit in (8, 16, 32) if bit < space_count]
    near_bits = [bit for bit in (1, 2, 4) if bit < space_count]
    positive_kx = upwind_sign > 0
    half_kx = kx_count // 2
    rank_pos = jnp.cumsum(positive_kx.astype(jnp.int32)) - 1
    rank_neg = jnp.cumsum((~positive_kx).astype(jnp.int32)) - 1
    slots = jnp.arange(half_kx, dtype=jnp.int32)
    pick_pos = (positive_kx[:, None] & (rank_pos[:, None] == slots[None, :])).astype(jnp.float32)
    pick_neg = ((~positive_kx)[:, None] & (rank_neg[:, None] == slots[None, :])).astype(jnp.float32)
    flat = distribution.reshape(-1, kx_count)
    send_right = jnp.dot(flat, pick_pos, precision=precise)
    send_left = jnp.dot(flat, pick_neg, precision=precise)
    forward_pairs = [(i, i + 1) for i in range(space_count - 1)]
    backward_pairs = [(i + 1, i) for i in range(space_count - 1)]
    got_left = lax.ppermute(send_right, "space", forward_pairs)
    got_right = lax.ppermute(send_left, "space", backward_pairs)
    far_rows = gather_rows(charge, "space", far_bits)
    held, far_rows, got_left, got_right = lax.optimization_barrier(
        (distribution, far_rows, got_left, got_right)
    )
    every_row = gather_rows(far_rows, "space", near_bits)
    every_row = in_row_order(every_row, far_bits + near_bits, space_count * row_count)
    every_row = sum_over(every_row, "ky", y_bits)
    density = lax.dynamic_slice_in_dim(every_row[:, 0], row_start, row_count, 0)
    every_row = every_row[:, 1]

    sine_rows = sine_table(grid_rows)
    sine_cols = sine_table(col_count)
    eigen_cols = eigen_values(col_count)
    along_x = jnp.dot(sine_rows, every_row, precision=precise)
    spectral = jnp.dot(along_x, sine_cols, precision=precise)
    spectral = spectral / (eigen_values(grid_rows)[:, None] + eigen_cols[None, :])
    back_cols = jnp.dot(spectral, sine_cols, precision=precise)
    own_rows = lax.dynamic_slice_in_dim(sine_rows, row_start, row_count, 0)
    potential = POISSON * jnp.dot(own_rows, back_cols, precision=precise)

    spread = lax.all_to_all(held, "ky", split_axis=2, concat_axis=1, tiled=True)
    local_cols = spread.shape[2]
    forward, backward = wigner_tables(ky_count)
    weights = own_differences(potential, ky_count, lax.axis_index("ky") * local_cols, local_cols)
    flattened = spread.reshape(row_count, ky_count, local_cols * kx_count)
    coeffs = jnp.einsum("ab,rbm->ram", forward, flattened, precision=triple)
    coeffs = coeffs.reshape(row_count, ky_count, local_cols, kx_count)
    scaled = coeffs * jnp.concatenate([weights, weights], axis=1)[..., None]
    mixed = jnp.einsum(
        "ab,rbm->ram",
        backward,
        scaled.reshape(row_count, ky_count, local_cols * kx_count),
        precision=triple,
    )
    mixed = mixed.reshape(row_count, ky_count, local_cols, kx_count)
    wigner = lax.all_to_all(mixed, "ky", split_axis=1, concat_axis=2, tiled=True)

    upstream_x = jnp.dot(got_left, pick_pos.T, precision=precise) + jnp.dot(
        got_right, pick_neg.T, precision=precise
    )
    upstream_x = upstream_x.reshape(distribution.shape)
    drift_x = -kx_speed[None, None, None, :] * (distribution - upstream_x)

    ky_global = lax.axis_index("ky") * ky_local + jnp.arange(ky_local, dtype=jnp.int32)
    upward = ky_global >= ky_count // 2
    vertical = DRIFT_Y * (ky_global.astype(jnp.float32) + 0.5 - 0.5 * ky_count) / (0.5 * ky_count)
    zero_col = jnp.zeros_like(distribution[:, :, :1])
    from_low = jnp.concatenate([zero_col, distribution[:, :, :-1]], axis=2)
    from_high = jnp.concatenate([distribution[:, :, 1:], zero_col], axis=2)
    upstream_y = jnp.where(upward[None, :, None, None], from_low, from_high)
    drift_y = -jnp.abs(vertical)[None, :, None, None] * (distribution - upstream_y)
    relaxation = relax_rate[:, None, :, None] * (
        density[:, None, :, None] * equilibrium[None, :, None, :] - distribution
    )
    base = distribution + STEP * (drift_x + drift_y + relaxation)
    wigner, base = lax.optimization_barrier((wigner, base))
    return base + STEP * wigner


def solution(mesh):
    return jax.shard_map(
        shards,
        mesh=mesh,
        in_specs=(
            P("space", "ky", None, None),
            P("space", None),
            P(),
            P(),
            P("ky", None),
            P(),
            P(),
        ),
        out_specs=P("space", "ky", None, None),
        check_vma=False,
    )
```

```python
import math

import jax
import jax.numpy as jnp
from jax import lax
from jax.sharding import PartitionSpec as P

COUPLING = 0.04
POISSON = 0.1
STEP = 0.4
DRIFT_Y = 0.8


def sine_table(length):
    positions = jnp.arange(1, length + 1, dtype=jnp.int32)
    phase_index = positions[:, None] * positions[None, :] % (2 * length + 2)
    return jnp.sqrt(2.0 / (length + 1.0)) * jnp.sin(
        math.pi * phase_index.astype(jnp.float32) / (length + 1.0)
    )


def eigen_values(length):
    positions = jnp.arange(1, length + 1, dtype=jnp.int32).astype(jnp.float32)
    return 4.0 * jnp.sin(0.5 * math.pi * positions / (length + 1.0)) ** 2


def wigner_tables(modes):
    half_count = modes // 2
    shifts = jnp.arange(1, half_count + 1, dtype=jnp.int32)
    wave_index = jnp.arange(modes, dtype=jnp.int32)
    phase_index = shifts[:, None] * wave_index[None, :] % modes
    angles = 2.0 * math.pi / modes * phase_index.astype(jnp.float32)
    forward = jnp.concatenate([jnp.cos(angles), jnp.sin(angles)], axis=0)
    backward = jnp.concatenate([jnp.sin(angles).T, -jnp.cos(angles).T], axis=1)
    return (forward, backward)


def own_differences(potential, modes, first_col, local_cols):
    half_count = modes // 2
    col_count = potential.shape[1]
    source = jnp.arange(col_count, dtype=jnp.int32)[:, None, None]
    shift = jnp.arange(1, half_count + 1, dtype=jnp.int32)[None, :, None]
    column = first_col + jnp.arange(local_cols, dtype=jnp.int32)[None, None, :]
    select = (source == column + shift).astype(jnp.float32) - (source == column - shift).astype(
        jnp.float32
    )
    picked = jnp.dot(
        potential,
        select.reshape(col_count, half_count * local_cols),
        precision=lax.Precision.HIGHEST,
    )
    return COUPLING * picked.reshape(potential.shape[0], half_count, local_cols)


def lookup(region, values_table):
    classes = jnp.arange(values_table.shape[0], dtype=jnp.int32)
    return jnp.sum(jnp.where(region[..., None] == classes, values_table, 0.0), axis=-1)


def xor_pairs(count, bit):
    return [(i, i ^ bit) for i in range(count)]


def sum_over(value, axis, bits):
    count = lax.axis_size(axis)
    for bit in bits:
        value = value + lax.ppermute(value, axis, xor_pairs(count, bit))
    return value


def gather_rows(value, axis, bits):
    count = lax.axis_size(axis)
    index = lax.axis_index(axis)
    for bit in bits:
        other = lax.ppermute(value, axis, xor_pairs(count, bit))
        low = (index & bit) == 0
        value = jnp.where(
            low, jnp.concatenate([value, other], 0), jnp.concatenate([other, value], 0)
        )
    return value


def in_row_order(value, bits, count):
    levels = len(bits)
    shaped = value.reshape((2,) * levels + (-1,) + value.shape[1:])
    order = sorted(range(levels), key=lambda axis: -bits[levels - 1 - axis])
    shaped = jnp.transpose(shaped, order + list(range(levels, shaped.ndim)))
    return shaped.reshape((count,) + value.shape[1:])


def select_exactly(values, picker):
    top = values.astype(jnp.bfloat16)
    remainder = values - top.astype(jnp.float32)
    middle = remainder.astype(jnp.bfloat16)
    rest = (remainder - middle.astype(jnp.float32)).astype(jnp.bfloat16)
    picker = picker.astype(jnp.bfloat16)
    total = jnp.dot(top, picker, preferred_element_type=jnp.float32)
    total = total + jnp.dot(middle, picker, preferred_element_type=jnp.float32)
    return total + jnp.dot(rest, picker, preferred_element_type=jnp.float32)


def shards(distribution, region, region_doping, region_relax, equilibrium, kx_speed, upwind_sign):
    precise = lax.Precision.HIGHEST
    triple = lax.Precision.HIGH
    row_count, ky_local, col_count, kx_count = distribution.shape
    ky_count = ky_local * lax.axis_size("ky")
    space_count = lax.axis_size("space")
    grid_rows = row_count * space_count
    space_index = lax.axis_index("space")
    row_start = space_index * row_count

    partial_value = jnp.sum(distribution, axis=(1, 3)) / (ky_count * kx_count)
    doping = lookup(region, region_doping)
    relax_rate = lookup(region, region_relax)
    ky_size = lax.axis_size("ky")
    z_bits = [ky_size // 2] if ky_size > 1 else []
    y_bits = [bit for bit in (1, 2, 4, 8, 16) if bit < ky_size // 2]
    partial_charge = partial_value - jnp.where(lax.axis_index("ky") == 0, doping, 0.0)
    charge = sum_over(jnp.stack([partial_value, partial_charge], axis=1), "ky", z_bits)
    far_bits = [bit for bit in (8, 16, 32) if bit < space_count]
    near_bits = [bit for bit in (1, 2, 4) if bit < space_count]
    positive_kx = upwind_sign > 0
    half_kx = kx_count // 2
    rank_pos = jnp.cumsum(positive_kx.astype(jnp.int32)) - 1
    rank_neg = jnp.cumsum((~positive_kx).astype(jnp.int32)) - 1
    slots = jnp.arange(half_kx, dtype=jnp.int32)
    pick_pos = (positive_kx[:, None] & (rank_pos[:, None] == slots[None, :])).astype(jnp.float32)
    pick_neg = ((~positive_kx)[:, None] & (rank_neg[:, None] == slots[None, :])).astype(jnp.float32)
    flat = distribution.reshape(-1, kx_count)
    send_right = select_exactly(flat, pick_pos)
    send_left = select_exactly(flat, pick_neg)
    forward_pairs = [(i, i + 1) for i in range(space_count - 1)]
    backward_pairs = [(i + 1, i) for i in range(space_count - 1)]
    got_left = lax.ppermute(send_right, "space", forward_pairs)
    got_right = lax.ppermute(send_left, "space", backward_pairs)
    far_rows = gather_rows(charge, "space", far_bits)
    held, far_rows, got_left, got_right = lax.optimization_barrier(
        (distribution, far_rows, got_left, got_right)
    )
    every_row = gather_rows(far_rows, "space", near_bits)
    every_row = in_row_order(every_row, far_bits + near_bits, space_count * row_count)
    every_row = sum_over(every_row, "ky", y_bits)
    density = lax.dynamic_slice_in_dim(every_row[:, 0], row_start, row_count, 0)
    every_row = every_row[:, 1]

    sine_rows = sine_table(grid_rows)
    sine_cols = sine_table(col_count)
    eigen_cols = eigen_values(col_count)
    along_x = jnp.dot(sine_rows, every_row, precision=precise)
    spectral = jnp.dot(along_x, sine_cols, precision=precise)
    spectral = spectral / (eigen_values(grid_rows)[:, None] + eigen_cols[None, :])
    back_cols = jnp.dot(spectral, sine_cols, precision=precise)
    own_rows = lax.dynamic_slice_in_dim(sine_rows, row_start, row_count, 0)
    potential = POISSON * jnp.dot(own_rows, back_cols, precision=precise)

    spread = lax.all_to_all(held, "ky", split_axis=2, concat_axis=1, tiled=True)
    local_cols = spread.shape[2]
    forward, backward = wigner_tables(ky_count)
    weights = own_differences(potential, ky_count, lax.axis_index("ky") * local_cols, local_cols)
    flattened = spread.reshape(row_count, ky_count, local_cols * kx_count)
    coeffs = jnp.einsum("ab,rbm->ram", forward, flattened, precision=triple)
    coeffs = coeffs.reshape(row_count, ky_count, local_cols, kx_count)
    scaled = coeffs * jnp.concatenate([weights, weights], axis=1)[..., None]
    mixed = jnp.einsum(
        "ab,rbm->ram",
        backward,
        scaled.reshape(row_count, ky_count, local_cols * kx_count),
        precision=triple,
    )
    mixed = mixed.reshape(row_count, ky_count, local_cols, kx_count)
    wigner = lax.all_to_all(mixed, "ky", split_axis=1, concat_axis=2, tiled=True)

    upstream_x = jnp.dot(got_left, pick_pos.T, precision=precise) + jnp.dot(
        got_right, pick_neg.T, precision=precise
    )
    upstream_x = upstream_x.reshape(distribution.shape)
    drift_x = -kx_speed[None, None, None, :] * (distribution - upstream_x)

    ky_global = lax.axis_index("ky") * ky_local + jnp.arange(ky_local, dtype=jnp.int32)
    upward = ky_global >= ky_count // 2
    vertical = DRIFT_Y * (ky_global.astype(jnp.float32) + 0.5 - 0.5 * ky_count) / (0.5 * ky_count)
    zero_col = jnp.zeros_like(distribution[:, :, :1])
    from_low = jnp.concatenate([zero_col, distribution[:, :, :-1]], axis=2)
    from_high = jnp.concatenate([distribution[:, :, 1:], zero_col], axis=2)
    upstream_y = jnp.where(upward[None, :, None, None], from_low, from_high)
    drift_y = -jnp.abs(vertical)[None, :, None, None] * (distribution - upstream_y)
    relaxation = relax_rate[:, None, :, None] * (
        density[:, None, :, None] * equilibrium[None, :, None, :] - distribution
    )
    base = distribution + STEP * (drift_x + drift_y + relaxation)
    wigner, base = lax.optimization_barrier((wigner, base))
    return base + STEP * wigner


def solution(mesh):
    return jax.shard_map(
        shards,
        mesh=mesh,
        in_specs=(
            P("space", "ky", None, None),
            P("space", None),
            P(),
            P(),
            P("ky", None),
            P(),
            P(),
        ),
        out_specs=P("space", "ky", None, None),
        check_vma=False,
    )
```

```python
import math

import jax
import jax.numpy as jnp
from jax import lax
from jax.sharding import PartitionSpec as P

COUPLING = 0.04
POISSON = 0.1
STEP = 0.4
DRIFT_Y = 0.8


def sine_table(length):
    positions = jnp.arange(1, length + 1, dtype=jnp.int32)
    phase_index = positions[:, None] * positions[None, :] % (2 * length + 2)
    return jnp.sqrt(2.0 / (length + 1.0)) * jnp.sin(
        math.pi * phase_index.astype(jnp.float32) / (length + 1.0)
    )


def eigen_values(length):
    positions = jnp.arange(1, length + 1, dtype=jnp.int32).astype(jnp.float32)
    return 4.0 * jnp.sin(0.5 * math.pi * positions / (length + 1.0)) ** 2


def wigner_tables(modes):
    half_count = modes // 2
    shifts = jnp.arange(1, half_count + 1, dtype=jnp.int32)
    wave_index = jnp.arange(modes, dtype=jnp.int32)
    phase_index = shifts[:, None] * wave_index[None, :] % modes
    angles = 2.0 * math.pi / modes * phase_index.astype(jnp.float32)
    forward = jnp.concatenate([jnp.cos(angles), jnp.sin(angles)], axis=0)
    backward = jnp.concatenate([jnp.sin(angles).T, -jnp.cos(angles).T], axis=1)
    return (forward, backward)


def own_differences(potential, modes, first_col, local_cols):
    half_count = modes // 2
    col_count = potential.shape[1]
    source = jnp.arange(col_count, dtype=jnp.int32)[:, None, None]
    shift = jnp.arange(1, half_count + 1, dtype=jnp.int32)[None, :, None]
    column = first_col + jnp.arange(local_cols, dtype=jnp.int32)[None, None, :]
    select = (source == column + shift).astype(jnp.float32) - (source == column - shift).astype(
        jnp.float32
    )
    picked = jnp.dot(
        potential,
        select.reshape(col_count, half_count * local_cols),
        precision=lax.Precision.HIGHEST,
    )
    return COUPLING * picked.reshape(potential.shape[0], half_count, local_cols)


def lookup(region, values_table):
    classes = jnp.arange(values_table.shape[0], dtype=jnp.int32)
    return jnp.sum(jnp.where(region[..., None] == classes, values_table, 0.0), axis=-1)


def xor_pairs(count, bit):
    return [(i, i ^ bit) for i in range(count)]


def sum_over(value, axis, bits):
    count = lax.axis_size(axis)
    for bit in bits:
        value = value + lax.ppermute(value, axis, xor_pairs(count, bit))
    return value


def gather_rows(value, axis, bits):
    count = lax.axis_size(axis)
    index = lax.axis_index(axis)
    for bit in bits:
        other = lax.ppermute(value, axis, xor_pairs(count, bit))
        low = (index & bit) == 0
        value = jnp.where(
            low, jnp.concatenate([value, other], 0), jnp.concatenate([other, value], 0)
        )
    return value


def in_row_order(value, bits, count):
    levels = len(bits)
    shaped = value.reshape((2,) * levels + (-1,) + value.shape[1:])
    order = sorted(range(levels), key=lambda axis: -bits[levels - 1 - axis])
    shaped = jnp.transpose(shaped, order + list(range(levels, shaped.ndim)))
    return shaped.reshape((count,) + value.shape[1:])


def shards(distribution, region, region_doping, region_relax, equilibrium, kx_speed, upwind_sign):
    precise = lax.Precision.HIGHEST
    triple = lax.Precision.HIGH
    row_count, ky_local, col_count, kx_count = distribution.shape
    ky_count = ky_local * lax.axis_size("ky")
    space_count = lax.axis_size("space")
    grid_rows = row_count * space_count
    space_index = lax.axis_index("space")
    row_start = space_index * row_count

    partial_value = jnp.sum(distribution, axis=(1, 3)) / (ky_count * kx_count)
    doping = lookup(region, region_doping)
    relax_rate = lookup(region, region_relax)
    ky_size = lax.axis_size("ky")
    z_bits = [ky_size // 2] if ky_size > 1 else []
    y_bits = [bit for bit in (1, 2, 4, 8, 16) if bit < ky_size // 2]
    partial_charge = partial_value - jnp.where(lax.axis_index("ky") == 0, doping, 0.0)
    charge = sum_over(jnp.stack([partial_value, partial_charge], axis=1), "ky", z_bits)
    far_bits = [bit for bit in (8, 16, 32) if bit < space_count]
    near_bits = [bit for bit in (1, 2, 4) if bit < space_count]
    far_rows = gather_rows(charge, "space", far_bits)
    held, far_rows = lax.optimization_barrier((distribution, far_rows))
    positive_kx = upwind_sign > 0
    half_kx = kx_count // 2
    rank_pos = jnp.cumsum(positive_kx.astype(jnp.int32)) - 1
    rank_neg = jnp.cumsum((~positive_kx).astype(jnp.int32)) - 1
    slots = jnp.arange(half_kx, dtype=jnp.int32)
    pick_pos = (positive_kx[:, None] & (rank_pos[:, None] == slots[None, :])).astype(jnp.float32)
    pick_neg = ((~positive_kx)[:, None] & (rank_neg[:, None] == slots[None, :])).astype(jnp.float32)
    flat = held.reshape(-1, kx_count)
    send_right = jnp.dot(flat, pick_pos, precision=precise)
    send_left = jnp.dot(flat, pick_neg, precision=precise)
    forward_pairs = [(i, i + 1) for i in range(space_count - 1)]
    backward_pairs = [(i + 1, i) for i in range(space_count - 1)]
    got_left = lax.ppermute(send_right, "space", forward_pairs)
    got_right = lax.ppermute(send_left, "space", backward_pairs)
    every_row = gather_rows(far_rows, "space", near_bits)
    every_row = in_row_order(every_row, far_bits + near_bits, space_count * row_count)
    every_row = sum_over(every_row, "ky", y_bits)
    density = lax.dynamic_slice_in_dim(every_row[:, 0], row_start, row_count, 0)
    every_row = every_row[:, 1]

    sine_rows = sine_table(grid_rows)
    sine_cols = sine_table(col_count)
    eigen_cols = eigen_values(col_count)
    along_x = jnp.dot(sine_rows, every_row, precision=precise)
    spectral = jnp.dot(along_x, sine_cols, precision=precise)
    spectral = spectral / (eigen_values(grid_rows)[:, None] + eigen_cols[None, :])
    back_cols = jnp.dot(spectral, sine_cols, precision=precise)
    own_rows = lax.dynamic_slice_in_dim(sine_rows, row_start, row_count, 0)
    potential = POISSON * jnp.dot(own_rows, back_cols, precision=precise)

    spread = lax.all_to_all(held, "ky", split_axis=2, concat_axis=1, tiled=True)
    local_cols = spread.shape[2]
    forward, backward = wigner_tables(ky_count)
    weights = own_differences(potential, ky_count, lax.axis_index("ky") * local_cols, local_cols)
    flattened = spread.reshape(row_count, ky_count, local_cols * kx_count)
    coeffs = jnp.einsum("ab,rbm->ram", forward, flattened, precision=triple)
    coeffs = coeffs.reshape(row_count, ky_count, local_cols, kx_count)
    scaled = coeffs * jnp.concatenate([weights, weights], axis=1)[..., None]
    mixed = jnp.einsum(
        "ab,rbm->ram",
        backward,
        scaled.reshape(row_count, ky_count, local_cols * kx_count),
        precision=triple,
    )
    mixed = mixed.reshape(row_count, ky_count, local_cols, kx_count)
    mixed, got_left, got_right = lax.optimization_barrier((mixed, got_left, got_right))
    wigner = lax.all_to_all(mixed, "ky", split_axis=1, concat_axis=2, tiled=True)

    upstream_x = jnp.dot(got_left, pick_pos.T, precision=precise) + jnp.dot(
        got_right, pick_neg.T, precision=precise
    )
    upstream_x = upstream_x.reshape(distribution.shape)
    drift_x = -kx_speed[None, None, None, :] * (distribution - upstream_x)

    ky_global = lax.axis_index("ky") * ky_local + jnp.arange(ky_local, dtype=jnp.int32)
    upward = ky_global >= ky_count // 2
    vertical = DRIFT_Y * (ky_global.astype(jnp.float32) + 0.5 - 0.5 * ky_count) / (0.5 * ky_count)
    zero_col = jnp.zeros_like(distribution[:, :, :1])
    from_low = jnp.concatenate([zero_col, distribution[:, :, :-1]], axis=2)
    from_high = jnp.concatenate([distribution[:, :, 1:], zero_col], axis=2)
    upstream_y = jnp.where(upward[None, :, None, None], from_low, from_high)
    drift_y = -jnp.abs(vertical)[None, :, None, None] * (distribution - upstream_y)
    relaxation = relax_rate[:, None, :, None] * (
        density[:, None, :, None] * equilibrium[None, :, None, :] - distribution
    )
    base = distribution + STEP * (drift_x + drift_y + relaxation)
    wigner, base = lax.optimization_barrier((wigner, base))
    return base + STEP * wigner


def solution(mesh):
    return jax.shard_map(
        shards,
        mesh=mesh,
        in_specs=(
            P("space", "ky", None, None),
            P("space", None),
            P(),
            P(),
            P("ky", None),
            P(),
            P(),
        ),
        out_specs=P("space", "ky", None, None),
        check_vma=False,
    )
```

```python
import math

import jax
import jax.numpy as jnp
from jax import lax
from jax.sharding import PartitionSpec as P

COUPLING = 0.04
POISSON = 0.1
STEP = 0.4
DRIFT_Y = 0.8


def sine_table(length):
    positions = jnp.arange(1, length + 1, dtype=jnp.int32)
    phase_index = positions[:, None] * positions[None, :] % (2 * length + 2)
    return jnp.sqrt(2.0 / (length + 1.0)) * jnp.sin(
        math.pi * phase_index.astype(jnp.float32) / (length + 1.0)
    )


def eigen_values(length):
    positions = jnp.arange(1, length + 1, dtype=jnp.int32).astype(jnp.float32)
    return 4.0 * jnp.sin(0.5 * math.pi * positions / (length + 1.0)) ** 2


def wigner_tables(modes):
    half_count = modes // 2
    shifts = jnp.arange(1, half_count + 1, dtype=jnp.int32)
    wave_index = jnp.arange(modes, dtype=jnp.int32)
    phase_index = shifts[:, None] * wave_index[None, :] % modes
    angles = 2.0 * math.pi / modes * phase_index.astype(jnp.float32)
    forward = jnp.concatenate([jnp.cos(angles), jnp.sin(angles)], axis=0)
    backward = jnp.concatenate([jnp.sin(angles).T, -jnp.cos(angles).T], axis=1)
    return (forward, backward)


def own_differences(potential, modes, first_col, local_cols):
    half_count = modes // 2
    col_count = potential.shape[1]
    source = jnp.arange(col_count, dtype=jnp.int32)[:, None, None]
    shift = jnp.arange(1, half_count + 1, dtype=jnp.int32)[None, :, None]
    column = first_col + jnp.arange(local_cols, dtype=jnp.int32)[None, None, :]
    select = (source == column + shift).astype(jnp.float32) - (source == column - shift).astype(
        jnp.float32
    )
    picked = jnp.dot(
        potential,
        select.reshape(col_count, half_count * local_cols),
        precision=lax.Precision.HIGHEST,
    )
    return COUPLING * picked.reshape(potential.shape[0], half_count, local_cols)


def lookup(region, values_table):
    classes = jnp.arange(values_table.shape[0], dtype=jnp.int32)
    return jnp.sum(jnp.where(region[..., None] == classes, values_table, 0.0), axis=-1)


def xor_pairs(count, bit):
    return [(i, i ^ bit) for i in range(count)]


def sum_over(value, axis, bits):
    count = lax.axis_size(axis)
    for bit in bits:
        value = value + lax.ppermute(value, axis, xor_pairs(count, bit))
    return value


def gather_rows(value, axis, bits):
    count = lax.axis_size(axis)
    index = lax.axis_index(axis)
    for bit in bits:
        other = lax.ppermute(value, axis, xor_pairs(count, bit))
        low = (index & bit) == 0
        value = jnp.where(
            low, jnp.concatenate([value, other], 0), jnp.concatenate([other, value], 0)
        )
    return value


def in_row_order(value, bits, count):
    levels = len(bits)
    shaped = value.reshape((2,) * levels + (-1,) + value.shape[1:])
    order = sorted(range(levels), key=lambda axis: -bits[levels - 1 - axis])
    shaped = jnp.transpose(shaped, order + list(range(levels, shaped.ndim)))
    return shaped.reshape((count,) + value.shape[1:])


def shards(distribution, region, region_doping, region_relax, equilibrium, kx_speed, upwind_sign):
    precise = lax.Precision.HIGHEST
    triple = lax.Precision.HIGH
    row_count, ky_local, col_count, kx_count = distribution.shape
    ky_count = ky_local * lax.axis_size("ky")
    space_count = lax.axis_size("space")
    grid_rows = row_count * space_count
    space_index = lax.axis_index("space")
    row_start = space_index * row_count

    partial_value = jnp.sum(distribution, axis=(1, 3)) / (ky_count * kx_count)
    doping = lookup(region, region_doping)
    relax_rate = lookup(region, region_relax)
    ky_size = lax.axis_size("ky")
    z_bits = [ky_size // 2] if ky_size > 1 else []
    y_bits = [bit for bit in (1, 2, 4, 8, 16) if bit < ky_size // 2]
    partial_charge = partial_value - jnp.where(lax.axis_index("ky") == 0, doping, 0.0)
    charge = jnp.stack([partial_value, partial_charge], axis=1)
    far_bits = [bit for bit in (8, 16, 32) if bit < space_count]
    near_bits = [bit for bit in (1, 2, 4) if bit < space_count]
    far_rows = gather_rows(charge, "space", far_bits)
    held, far_rows = lax.optimization_barrier((distribution, far_rows))
    positive_kx = upwind_sign > 0
    half_kx = kx_count // 2
    rank_pos = jnp.cumsum(positive_kx.astype(jnp.int32)) - 1
    rank_neg = jnp.cumsum((~positive_kx).astype(jnp.int32)) - 1
    slots = jnp.arange(half_kx, dtype=jnp.int32)
    pick_pos = (positive_kx[:, None] & (rank_pos[:, None] == slots[None, :])).astype(jnp.float32)
    pick_neg = ((~positive_kx)[:, None] & (rank_neg[:, None] == slots[None, :])).astype(jnp.float32)
    flat = held.reshape(-1, kx_count)
    send_right = jnp.dot(flat, pick_pos, precision=precise)
    send_left = jnp.dot(flat, pick_neg, precision=precise)
    forward_pairs = [(i, i + 1) for i in range(space_count - 1)]
    backward_pairs = [(i + 1, i) for i in range(space_count - 1)]
    got_left = lax.ppermute(send_right, "space", forward_pairs)
    got_right = lax.ppermute(send_left, "space", backward_pairs)
    every_row = gather_rows(far_rows, "space", near_bits)
    every_row = in_row_order(every_row, far_bits + near_bits, space_count * row_count)
    every_row = sum_over(every_row, "ky", y_bits + z_bits)
    density = lax.dynamic_slice_in_dim(every_row[:, 0], row_start, row_count, 0)
    every_row = every_row[:, 1]

    sine_rows = sine_table(grid_rows)
    sine_cols = sine_table(col_count)
    eigen_cols = eigen_values(col_count)
    along_x = jnp.dot(sine_rows, every_row, precision=precise)
    spectral = jnp.dot(along_x, sine_cols, precision=precise)
    spectral = spectral / (eigen_values(grid_rows)[:, None] + eigen_cols[None, :])
    back_cols = jnp.dot(spectral, sine_cols, precision=precise)
    own_rows = lax.dynamic_slice_in_dim(sine_rows, row_start, row_count, 0)
    potential = POISSON * jnp.dot(own_rows, back_cols, precision=precise)

    spread = lax.all_to_all(held, "ky", split_axis=2, concat_axis=1, tiled=True)
    local_cols = spread.shape[2]
    forward, backward = wigner_tables(ky_count)
    weights = own_differences(potential, ky_count, lax.axis_index("ky") * local_cols, local_cols)
    flattened = spread.reshape(row_count, ky_count, local_cols * kx_count)
    coeffs = jnp.einsum("ab,rbm->ram", forward, flattened, precision=triple)
    coeffs = coeffs.reshape(row_count, ky_count, local_cols, kx_count)
    scaled = coeffs * jnp.concatenate([weights, weights], axis=1)[..., None]
    mixed = jnp.einsum(
        "ab,rbm->ram",
        backward,
        scaled.reshape(row_count, ky_count, local_cols * kx_count),
        precision=triple,
    )
    mixed = mixed.reshape(row_count, ky_count, local_cols, kx_count)
    mixed, got_left, got_right = lax.optimization_barrier((mixed, got_left, got_right))
    wigner = lax.all_to_all(mixed, "ky", split_axis=1, concat_axis=2, tiled=True)

    upstream_x = jnp.dot(got_left, pick_pos.T, precision=precise) + jnp.dot(
        got_right, pick_neg.T, precision=precise
    )
    upstream_x = upstream_x.reshape(distribution.shape)
    drift_x = -kx_speed[None, None, None, :] * (distribution - upstream_x)

    ky_global = lax.axis_index("ky") * ky_local + jnp.arange(ky_local, dtype=jnp.int32)
    upward = ky_global >= ky_count // 2
    vertical = DRIFT_Y * (ky_global.astype(jnp.float32) + 0.5 - 0.5 * ky_count) / (0.5 * ky_count)
    zero_col = jnp.zeros_like(distribution[:, :, :1])
    from_low = jnp.concatenate([zero_col, distribution[:, :, :-1]], axis=2)
    from_high = jnp.concatenate([distribution[:, :, 1:], zero_col], axis=2)
    upstream_y = jnp.where(upward[None, :, None, None], from_low, from_high)
    drift_y = -jnp.abs(vertical)[None, :, None, None] * (distribution - upstream_y)
    relaxation = relax_rate[:, None, :, None] * (
        density[:, None, :, None] * equilibrium[None, :, None, :] - distribution
    )
    base = distribution + STEP * (drift_x + drift_y + relaxation)
    wigner, base = lax.optimization_barrier((wigner, base))
    return base + STEP * wigner


def solution(mesh):
    return jax.shard_map(
        shards,
        mesh=mesh,
        in_specs=(
            P("space", "ky", None, None),
            P("space", None),
            P(),
            P(),
            P("ky", None),
            P(),
            P(),
        ),
        out_specs=P("space", "ky", None, None),
        check_vma=False,
    )
```

```python
import math

import jax
import jax.numpy as jnp
from jax import lax
from jax.sharding import PartitionSpec as P

COUPLING = 0.04
POISSON = 0.1
STEP = 0.4
DRIFT_Y = 0.8


def sine_table(length):
    positions = jnp.arange(1, length + 1, dtype=jnp.int32)
    phase_index = positions[:, None] * positions[None, :] % (2 * length + 2)
    return jnp.sqrt(2.0 / (length + 1.0)) * jnp.sin(
        math.pi * phase_index.astype(jnp.float32) / (length + 1.0)
    )


def eigen_values(length):
    positions = jnp.arange(1, length + 1, dtype=jnp.int32).astype(jnp.float32)
    return 4.0 * jnp.sin(0.5 * math.pi * positions / (length + 1.0)) ** 2


def wigner_tables(modes):
    half_count = modes // 2
    shifts = jnp.arange(1, half_count + 1, dtype=jnp.int32)
    wave_index = jnp.arange(modes, dtype=jnp.int32)
    phase_index = shifts[:, None] * wave_index[None, :] % modes
    angles = 2.0 * math.pi / modes * phase_index.astype(jnp.float32)
    forward = jnp.concatenate([jnp.cos(angles), jnp.sin(angles)], axis=0)
    backward = jnp.concatenate([jnp.sin(angles).T, -jnp.cos(angles).T], axis=1)
    return (forward, backward)


def own_differences(potential, modes, first_col, local_cols):
    half_count = modes // 2
    col_count = potential.shape[1]
    source = jnp.arange(col_count, dtype=jnp.int32)[:, None, None]
    shift = jnp.arange(1, half_count + 1, dtype=jnp.int32)[None, :, None]
    column = first_col + jnp.arange(local_cols, dtype=jnp.int32)[None, None, :]
    select = (source == column + shift).astype(jnp.float32) - (source == column - shift).astype(
        jnp.float32
    )
    picked = jnp.dot(
        potential,
        select.reshape(col_count, half_count * local_cols),
        precision=lax.Precision.HIGHEST,
    )
    return COUPLING * picked.reshape(potential.shape[0], half_count, local_cols)


def lookup(region, values_table):
    classes = jnp.arange(values_table.shape[0], dtype=jnp.int32)
    return jnp.sum(jnp.where(region[..., None] == classes, values_table, 0.0), axis=-1)


def xor_pairs(count, bit):
    return [(i, i ^ bit) for i in range(count)]


def sum_over(value, axis, bits):
    count = lax.axis_size(axis)
    for bit in bits:
        value = value + lax.ppermute(value, axis, xor_pairs(count, bit))
    return value


def gather_rows(value, axis, bits):
    count = lax.axis_size(axis)
    index = lax.axis_index(axis)
    for bit in bits:
        other = lax.ppermute(value, axis, xor_pairs(count, bit))
        low = (index & bit) == 0
        value = jnp.where(
            low, jnp.concatenate([value, other], 0), jnp.concatenate([other, value], 0)
        )
    return value


def in_row_order(value, bits, count):
    levels = len(bits)
    shaped = value.reshape((2,) * levels + (-1,) + value.shape[1:])
    order = sorted(range(levels), key=lambda axis: -bits[levels - 1 - axis])
    shaped = jnp.transpose(shaped, order + list(range(levels, shaped.ndim)))
    return shaped.reshape((count,) + value.shape[1:])


def spread_by_shifts(block):
    ky_size = lax.axis_size("ky")
    index = lax.axis_index("ky")
    rows, ky_local, col_count, kx_count = block.shape
    width = col_count // ky_size
    blocks = block.reshape(rows, ky_local, ky_size, width, kx_count)
    received = []
    for shift in range(ky_size):
        piece = lax.dynamic_index_in_dim(blocks, (index + shift) % ky_size, 2, keepdims=False)
        if shift:
            pairs = [(i, (i + shift) % ky_size) for i in range(ky_size)]
            piece = lax.ppermute(piece, "ky", pairs)
        received.append(piece)
    stacked = jnp.stack(received, 0)
    stacked = jnp.take(stacked, (index - jnp.arange(ky_size)) % ky_size, axis=0)
    stacked = jnp.moveaxis(stacked, 0, 1)
    return stacked.reshape(rows, ky_size * ky_local, width, kx_count)


def shards(distribution, region, region_doping, region_relax, equilibrium, kx_speed, upwind_sign):
    precise = lax.Precision.HIGHEST
    triple = lax.Precision.HIGH
    row_count, ky_local, col_count, kx_count = distribution.shape
    ky_count = ky_local * lax.axis_size("ky")
    space_count = lax.axis_size("space")
    grid_rows = row_count * space_count
    space_index = lax.axis_index("space")
    row_start = space_index * row_count

    partial_value = jnp.sum(distribution, axis=(1, 3)) / (ky_count * kx_count)
    doping = lookup(region, region_doping)
    relax_rate = lookup(region, region_relax)
    ky_size = lax.axis_size("ky")
    z_bits = [ky_size // 2] if ky_size > 1 else []
    y_bits = [bit for bit in (1, 2, 4, 8, 16) if bit < ky_size // 2]
    partial_charge = partial_value - jnp.where(lax.axis_index("ky") == 0, doping, 0.0)
    charge = sum_over(jnp.stack([partial_value, partial_charge], axis=1), "ky", z_bits)
    far_bits = [bit for bit in (8, 16, 32) if bit < space_count]
    near_bits = [bit for bit in (1, 2, 4) if bit < space_count]
    far_rows = gather_rows(charge, "space", far_bits)
    held, far_rows = lax.optimization_barrier((distribution, far_rows))
    positive_kx = upwind_sign > 0
    half_kx = kx_count // 2
    rank_pos = jnp.cumsum(positive_kx.astype(jnp.int32)) - 1
    rank_neg = jnp.cumsum((~positive_kx).astype(jnp.int32)) - 1
    slots = jnp.arange(half_kx, dtype=jnp.int32)
    pick_pos = (positive_kx[:, None] & (rank_pos[:, None] == slots[None, :])).astype(jnp.float32)
    pick_neg = ((~positive_kx)[:, None] & (rank_neg[:, None] == slots[None, :])).astype(jnp.float32)
    flat = held.reshape(-1, kx_count)
    send_right = jnp.dot(flat, pick_pos, precision=precise)
    send_left = jnp.dot(flat, pick_neg, precision=precise)
    forward_pairs = [(i, i + 1) for i in range(space_count - 1)]
    backward_pairs = [(i + 1, i) for i in range(space_count - 1)]
    got_left = lax.ppermute(send_right, "space", forward_pairs)
    got_right = lax.ppermute(send_left, "space", backward_pairs)
    every_row = gather_rows(far_rows, "space", near_bits)
    every_row = in_row_order(every_row, far_bits + near_bits, space_count * row_count)
    every_row = sum_over(every_row, "ky", y_bits)
    density = lax.dynamic_slice_in_dim(every_row[:, 0], row_start, row_count, 0)
    every_row = every_row[:, 1]

    sine_rows = sine_table(grid_rows)
    sine_cols = sine_table(col_count)
    eigen_cols = eigen_values(col_count)
    along_x = jnp.dot(sine_rows, every_row, precision=precise)
    spectral = jnp.dot(along_x, sine_cols, precision=precise)
    spectral = spectral / (eigen_values(grid_rows)[:, None] + eigen_cols[None, :])
    back_cols = jnp.dot(spectral, sine_cols, precision=precise)
    own_rows = lax.dynamic_slice_in_dim(sine_rows, row_start, row_count, 0)
    potential = POISSON * jnp.dot(own_rows, back_cols, precision=precise)

    spread = spread_by_shifts(held)
    local_cols = spread.shape[2]
    forward, backward = wigner_tables(ky_count)
    weights = own_differences(potential, ky_count, lax.axis_index("ky") * local_cols, local_cols)
    flattened = spread.reshape(row_count, ky_count, local_cols * kx_count)
    coeffs = jnp.einsum("ab,rbm->ram", forward, flattened, precision=triple)
    coeffs = coeffs.reshape(row_count, ky_count, local_cols, kx_count)
    scaled = coeffs * jnp.concatenate([weights, weights], axis=1)[..., None]
    mixed = jnp.einsum(
        "ab,rbm->ram",
        backward,
        scaled.reshape(row_count, ky_count, local_cols * kx_count),
        precision=triple,
    )
    mixed = mixed.reshape(row_count, ky_count, local_cols, kx_count)
    mixed, got_left, got_right = lax.optimization_barrier((mixed, got_left, got_right))
    wigner = lax.all_to_all(mixed, "ky", split_axis=1, concat_axis=2, tiled=True)

    upstream_x = jnp.dot(got_left, pick_pos.T, precision=precise) + jnp.dot(
        got_right, pick_neg.T, precision=precise
    )
    upstream_x = upstream_x.reshape(distribution.shape)
    drift_x = -kx_speed[None, None, None, :] * (distribution - upstream_x)

    ky_global = lax.axis_index("ky") * ky_local + jnp.arange(ky_local, dtype=jnp.int32)
    upward = ky_global >= ky_count // 2
    vertical = DRIFT_Y * (ky_global.astype(jnp.float32) + 0.5 - 0.5 * ky_count) / (0.5 * ky_count)
    zero_col = jnp.zeros_like(distribution[:, :, :1])
    from_low = jnp.concatenate([zero_col, distribution[:, :, :-1]], axis=2)
    from_high = jnp.concatenate([distribution[:, :, 1:], zero_col], axis=2)
    upstream_y = jnp.where(upward[None, :, None, None], from_low, from_high)
    drift_y = -jnp.abs(vertical)[None, :, None, None] * (distribution - upstream_y)
    relaxation = relax_rate[:, None, :, None] * (
        density[:, None, :, None] * equilibrium[None, :, None, :] - distribution
    )
    base = distribution + STEP * (drift_x + drift_y + relaxation)
    wigner, base = lax.optimization_barrier((wigner, base))
    return base + STEP * wigner


def solution(mesh):
    return jax.shard_map(
        shards,
        mesh=mesh,
        in_specs=(
            P("space", "ky", None, None),
            P("space", None),
            P(),
            P(),
            P("ky", None),
            P(),
            P(),
        ),
        out_specs=P("space", "ky", None, None),
        check_vma=False,
    )
```

```python
import math

import jax
import jax.numpy as jnp
from jax import lax
from jax.sharding import PartitionSpec as P

COUPLING = 0.04
POISSON = 0.1
STEP = 0.4
DRIFT_Y = 0.8


def sine_table(length):
    positions = jnp.arange(1, length + 1, dtype=jnp.int32)
    phase_index = positions[:, None] * positions[None, :] % (2 * length + 2)
    return jnp.sqrt(2.0 / (length + 1.0)) * jnp.sin(
        math.pi * phase_index.astype(jnp.float32) / (length + 1.0)
    )


def eigen_values(length):
    positions = jnp.arange(1, length + 1, dtype=jnp.int32).astype(jnp.float32)
    return 4.0 * jnp.sin(0.5 * math.pi * positions / (length + 1.0)) ** 2


def wigner_tables(modes):
    half_count = modes // 2
    shifts = jnp.arange(1, half_count + 1, dtype=jnp.int32)
    wave_index = jnp.arange(modes, dtype=jnp.int32)
    phase_index = shifts[:, None] * wave_index[None, :] % modes
    angles = 2.0 * math.pi / modes * phase_index.astype(jnp.float32)
    forward = jnp.concatenate([jnp.cos(angles), jnp.sin(angles)], axis=0)
    backward = jnp.concatenate([jnp.sin(angles).T, -jnp.cos(angles).T], axis=1)
    return (forward, backward)


def own_differences(potential, modes, first_col, local_cols):
    half_count = modes // 2
    col_count = potential.shape[1]
    source = jnp.arange(col_count, dtype=jnp.int32)[:, None, None]
    shift = jnp.arange(1, half_count + 1, dtype=jnp.int32)[None, :, None]
    column = first_col + jnp.arange(local_cols, dtype=jnp.int32)[None, None, :]
    select = (source == column + shift).astype(jnp.float32) - (source == column - shift).astype(
        jnp.float32
    )
    picked = jnp.dot(
        potential,
        select.reshape(col_count, half_count * local_cols),
        precision=lax.Precision.HIGHEST,
    )
    return COUPLING * picked.reshape(potential.shape[0], half_count, local_cols)


def lookup(region, values_table):
    classes = jnp.arange(values_table.shape[0], dtype=jnp.int32)
    return jnp.sum(jnp.where(region[..., None] == classes, values_table, 0.0), axis=-1)


def xor_pairs(count, bit):
    return [(i, i ^ bit) for i in range(count)]


def sum_over(value, axis, bits):
    count = lax.axis_size(axis)
    for bit in bits:
        value = value + lax.ppermute(value, axis, xor_pairs(count, bit))
    return value


def gather_rows(value, axis, bits):
    count = lax.axis_size(axis)
    index = lax.axis_index(axis)
    for bit in bits:
        other = lax.ppermute(value, axis, xor_pairs(count, bit))
        low = (index & bit) == 0
        value = jnp.where(
            low, jnp.concatenate([value, other], 0), jnp.concatenate([other, value], 0)
        )
    return value


def in_row_order(value, bits, count):
    levels = len(bits)
    shaped = value.reshape((2,) * levels + (-1,) + value.shape[1:])
    order = sorted(range(levels), key=lambda axis: -bits[levels - 1 - axis])
    shaped = jnp.transpose(shaped, order + list(range(levels, shaped.ndim)))
    return shaped.reshape((count,) + value.shape[1:])


def shards(distribution, region, region_doping, region_relax, equilibrium, kx_speed, upwind_sign):
    precise = lax.Precision.HIGHEST
    triple = lax.Precision.HIGH
    row_count, ky_local, col_count, kx_count = distribution.shape
    ky_count = ky_local * lax.axis_size("ky")
    space_count = lax.axis_size("space")
    grid_rows = row_count * space_count
    space_index = lax.axis_index("space")
    row_start = space_index * row_count

    partial_value = jnp.sum(distribution, axis=(1, 3)) / (ky_count * kx_count)
    doping = lookup(region, region_doping)
    relax_rate = lookup(region, region_relax)
    ky_size = lax.axis_size("ky")
    z_bits = [ky_size // 2] if ky_size > 1 else []
    y_bits = [bit for bit in (1, 2, 4, 8, 16) if bit < ky_size // 2]
    partial_charge = partial_value - jnp.where(lax.axis_index("ky") == 0, doping, 0.0)
    charge = sum_over(jnp.stack([partial_value, partial_charge], axis=1), "ky", z_bits)
    far_bits = [bit for bit in (8, 16, 32) if bit < space_count]
    near_bits = [bit for bit in (1, 2, 4) if bit < space_count]
    far_rows = gather_rows(charge, "space", far_bits)
    positive_kx = upwind_sign > 0
    half_kx = kx_count // 2
    rank_pos = jnp.cumsum(positive_kx.astype(jnp.int32)) - 1
    rank_neg = jnp.cumsum((~positive_kx).astype(jnp.int32)) - 1
    slots = jnp.arange(half_kx, dtype=jnp.int32)
    pick_pos = (positive_kx[:, None] & (rank_pos[:, None] == slots[None, :])).astype(jnp.float32)
    pick_neg = ((~positive_kx)[:, None] & (rank_neg[:, None] == slots[None, :])).astype(jnp.float32)
    flat = distribution.reshape(-1, kx_count)
    send_right = jnp.dot(flat, pick_pos, precision=precise)
    send_left = jnp.dot(flat, pick_neg, precision=precise)
    held, far_rows, send_right, send_left = lax.optimization_barrier(
        (distribution, far_rows, send_right, send_left)
    )
    forward_pairs = [(i, i + 1) for i in range(space_count - 1)]
    backward_pairs = [(i + 1, i) for i in range(space_count - 1)]
    got_left = lax.ppermute(send_right, "space", forward_pairs)
    got_right = lax.ppermute(send_left, "space", backward_pairs)
    every_row = gather_rows(far_rows, "space", near_bits)
    every_row = in_row_order(every_row, far_bits + near_bits, space_count * row_count)
    every_row = sum_over(every_row, "ky", y_bits)
    density = lax.dynamic_slice_in_dim(every_row[:, 0], row_start, row_count, 0)
    every_row = every_row[:, 1]

    sine_rows = sine_table(grid_rows)
    sine_cols = sine_table(col_count)
    eigen_cols = eigen_values(col_count)
    along_x = jnp.dot(sine_rows, every_row, precision=precise)
    spectral = jnp.dot(along_x, sine_cols, precision=precise)
    spectral = spectral / (eigen_values(grid_rows)[:, None] + eigen_cols[None, :])
    back_cols = jnp.dot(spectral, sine_cols, precision=precise)
    own_rows = lax.dynamic_slice_in_dim(sine_rows, row_start, row_count, 0)
    potential = POISSON * jnp.dot(own_rows, back_cols, precision=precise)

    spread = lax.all_to_all(held, "ky", split_axis=2, concat_axis=1, tiled=True)
    local_cols = spread.shape[2]
    forward, backward = wigner_tables(ky_count)
    weights = own_differences(potential, ky_count, lax.axis_index("ky") * local_cols, local_cols)
    flattened = spread.reshape(row_count, ky_count, local_cols * kx_count)
    coeffs = jnp.einsum("ab,rbm->ram", forward, flattened, precision=triple)
    coeffs = coeffs.reshape(row_count, ky_count, local_cols, kx_count)
    scaled = coeffs * jnp.concatenate([weights, weights], axis=1)[..., None]
    mixed = jnp.einsum(
        "ab,rbm->ram",
        backward,
        scaled.reshape(row_count, ky_count, local_cols * kx_count),
        precision=triple,
    )
    mixed = mixed.reshape(row_count, ky_count, local_cols, kx_count)
    mixed, got_left, got_right = lax.optimization_barrier((mixed, got_left, got_right))
    wigner = lax.all_to_all(mixed, "ky", split_axis=1, concat_axis=2, tiled=True)

    upstream_x = jnp.dot(got_left, pick_pos.T, precision=precise) + jnp.dot(
        got_right, pick_neg.T, precision=precise
    )
    upstream_x = upstream_x.reshape(distribution.shape)
    drift_x = -kx_speed[None, None, None, :] * (distribution - upstream_x)

    ky_global = lax.axis_index("ky") * ky_local + jnp.arange(ky_local, dtype=jnp.int32)
    upward = ky_global >= ky_count // 2
    vertical = DRIFT_Y * (ky_global.astype(jnp.float32) + 0.5 - 0.5 * ky_count) / (0.5 * ky_count)
    zero_col = jnp.zeros_like(distribution[:, :, :1])
    from_low = jnp.concatenate([zero_col, distribution[:, :, :-1]], axis=2)
    from_high = jnp.concatenate([distribution[:, :, 1:], zero_col], axis=2)
    upstream_y = jnp.where(upward[None, :, None, None], from_low, from_high)
    drift_y = -jnp.abs(vertical)[None, :, None, None] * (distribution - upstream_y)
    relaxation = relax_rate[:, None, :, None] * (
        density[:, None, :, None] * equilibrium[None, :, None, :] - distribution
    )
    base = distribution + STEP * (drift_x + drift_y + relaxation)
    wigner, base = lax.optimization_barrier((wigner, base))
    return base + STEP * wigner


def solution(mesh):
    return jax.shard_map(
        shards,
        mesh=mesh,
        in_specs=(
            P("space", "ky", None, None),
            P("space", None),
            P(),
            P(),
            P("ky", None),
            P(),
            P(),
        ),
        out_specs=P("space", "ky", None, None),
        check_vma=False,
    )
```

```python
import math

import jax
import jax.numpy as jnp
from jax import lax
from jax.sharding import PartitionSpec as P

COUPLING = 0.04
POISSON = 0.1
STEP = 0.4
DRIFT_Y = 0.8


def sine_table(length):
    positions = jnp.arange(1, length + 1, dtype=jnp.int32)
    phase_index = positions[:, None] * positions[None, :] % (2 * length + 2)
    return jnp.sqrt(2.0 / (length + 1.0)) * jnp.sin(
        math.pi * phase_index.astype(jnp.float32) / (length + 1.0)
    )


def eigen_values(length):
    positions = jnp.arange(1, length + 1, dtype=jnp.int32).astype(jnp.float32)
    return 4.0 * jnp.sin(0.5 * math.pi * positions / (length + 1.0)) ** 2


def wigner_tables(modes):
    half_count = modes // 2
    shifts = jnp.arange(1, half_count + 1, dtype=jnp.int32)
    wave_index = jnp.arange(modes, dtype=jnp.int32)
    phase_index = shifts[:, None] * wave_index[None, :] % modes
    angles = 2.0 * math.pi / modes * phase_index.astype(jnp.float32)
    forward = jnp.concatenate([jnp.cos(angles), jnp.sin(angles)], axis=0)
    backward = jnp.concatenate([jnp.sin(angles).T, -jnp.cos(angles).T], axis=1)
    return (forward, backward)


def own_differences(potential, modes, first_col, local_cols):
    half_count = modes // 2
    col_count = potential.shape[1]
    source = jnp.arange(col_count, dtype=jnp.int32)[:, None, None]
    shift = jnp.arange(1, half_count + 1, dtype=jnp.int32)[None, :, None]
    column = first_col + jnp.arange(local_cols, dtype=jnp.int32)[None, None, :]
    select = (source == column + shift).astype(jnp.float32) - (source == column - shift).astype(
        jnp.float32
    )
    picked = jnp.dot(
        potential,
        select.reshape(col_count, half_count * local_cols),
        precision=lax.Precision.HIGHEST,
    )
    return COUPLING * picked.reshape(potential.shape[0], half_count, local_cols)


def lookup(region, values_table):
    classes = jnp.arange(values_table.shape[0], dtype=jnp.int32)
    return jnp.sum(jnp.where(region[..., None] == classes, values_table, 0.0), axis=-1)


def xor_pairs(count, bit):
    return [(i, i ^ bit) for i in range(count)]


def sum_over(value, axis, bits):
    count = lax.axis_size(axis)
    for bit in bits:
        value = value + lax.ppermute(value, axis, xor_pairs(count, bit))
    return value


def gather_rows(value, axis, bits):
    count = lax.axis_size(axis)
    index = lax.axis_index(axis)
    for bit in bits:
        other = lax.ppermute(value, axis, xor_pairs(count, bit))
        low = (index & bit) == 0
        value = jnp.where(
            low, jnp.concatenate([value, other], 0), jnp.concatenate([other, value], 0)
        )
    return value


def in_row_order(value, bits, count):
    levels = len(bits)
    shaped = value.reshape((2,) * levels + (-1,) + value.shape[1:])
    order = sorted(range(levels), key=lambda axis: -bits[levels - 1 - axis])
    shaped = jnp.transpose(shaped, order + list(range(levels, shaped.ndim)))
    return shaped.reshape((count,) + value.shape[1:])


def shards(distribution, region, region_doping, region_relax, equilibrium, kx_speed, upwind_sign):
    precise = lax.Precision.HIGHEST
    triple = lax.Precision.HIGH
    row_count, ky_local, col_count, kx_count = distribution.shape
    ky_count = ky_local * lax.axis_size("ky")
    space_count = lax.axis_size("space")
    grid_rows = row_count * space_count
    space_index = lax.axis_index("space")
    row_start = space_index * row_count

    partial_value = jnp.sum(distribution, axis=(1, 3)) / (ky_count * kx_count)
    doping = lookup(region, region_doping)
    relax_rate = lookup(region, region_relax)
    ky_size = lax.axis_size("ky")
    z_bits = [ky_size // 2] if ky_size > 1 else []
    y_bits = [bit for bit in (1, 2, 4, 8, 16) if bit < ky_size // 2]
    partial_charge = partial_value - jnp.where(lax.axis_index("ky") == 0, doping, 0.0)
    charge = sum_over(jnp.stack([partial_value, partial_charge], axis=1), "ky", z_bits)
    far_bits = [bit for bit in (8, 16, 32) if bit < space_count]
    near_bits = [bit for bit in (1, 2, 4) if bit < space_count]
    far_rows = gather_rows(charge, "space", far_bits)
    held, far_rows = lax.optimization_barrier((distribution, far_rows))
    positive_kx = upwind_sign > 0
    half_kx = kx_count // 2
    rank_pos = jnp.cumsum(positive_kx.astype(jnp.int32)) - 1
    rank_neg = jnp.cumsum((~positive_kx).astype(jnp.int32)) - 1
    slots = jnp.arange(half_kx, dtype=jnp.int32)
    pick_pos = (positive_kx[:, None] & (rank_pos[:, None] == slots[None, :])).astype(jnp.float32)
    pick_neg = ((~positive_kx)[:, None] & (rank_neg[:, None] == slots[None, :])).astype(jnp.float32)
    flat = held.reshape(-1, kx_count)
    send_right = jnp.dot(flat, pick_pos, precision=precise)
    send_left = jnp.dot(flat, pick_neg, precision=precise)
    forward_pairs = [(i, i + 1) for i in range(space_count - 1)]
    backward_pairs = [(i + 1, i) for i in range(space_count - 1)]
    got_left = lax.ppermute(send_right, "space", forward_pairs)
    got_right = lax.ppermute(send_left, "space", backward_pairs)
    far_rows, got_left, got_right = lax.optimization_barrier((far_rows, got_left, got_right))
    every_row = gather_rows(far_rows, "space", near_bits)
    every_row = in_row_order(every_row, far_bits + near_bits, space_count * row_count)
    every_row = sum_over(every_row, "ky", y_bits)
    density = lax.dynamic_slice_in_dim(every_row[:, 0], row_start, row_count, 0)
    every_row = every_row[:, 1]

    sine_rows = sine_table(grid_rows)
    sine_cols = sine_table(col_count)
    eigen_cols = eigen_values(col_count)
    along_x = jnp.dot(sine_rows, every_row, precision=precise)
    spectral = jnp.dot(along_x, sine_cols, precision=precise)
    spectral = spectral / (eigen_values(grid_rows)[:, None] + eigen_cols[None, :])
    back_cols = jnp.dot(spectral, sine_cols, precision=precise)
    own_rows = lax.dynamic_slice_in_dim(sine_rows, row_start, row_count, 0)
    potential = POISSON * jnp.dot(own_rows, back_cols, precision=precise)

    spread = lax.all_to_all(held, "ky", split_axis=2, concat_axis=1, tiled=True)
    local_cols = spread.shape[2]
    forward, backward = wigner_tables(ky_count)
    weights = own_differences(potential, ky_count, lax.axis_index("ky") * local_cols, local_cols)
    flattened = spread.reshape(row_count, ky_count, local_cols * kx_count)
    coeffs = jnp.einsum("ab,rbm->ram", forward, flattened, precision=triple)
    coeffs = coeffs.reshape(row_count, ky_count, local_cols, kx_count)
    scaled = coeffs * jnp.concatenate([weights, weights], axis=1)[..., None]
    mixed = jnp.einsum(
        "ab,rbm->ram",
        backward,
        scaled.reshape(row_count, ky_count, local_cols * kx_count),
        precision=triple,
    )
    mixed = mixed.reshape(row_count, ky_count, local_cols, kx_count)
    mixed, got_left, got_right = lax.optimization_barrier((mixed, got_left, got_right))
    wigner = lax.all_to_all(mixed, "ky", split_axis=1, concat_axis=2, tiled=True)

    upstream_x = jnp.dot(got_left, pick_pos.T, precision=precise) + jnp.dot(
        got_right, pick_neg.T, precision=precise
    )
    upstream_x = upstream_x.reshape(distribution.shape)
    drift_x = -kx_speed[None, None, None, :] * (distribution - upstream_x)

    ky_global = lax.axis_index("ky") * ky_local + jnp.arange(ky_local, dtype=jnp.int32)
    upward = ky_global >= ky_count // 2
    vertical = DRIFT_Y * (ky_global.astype(jnp.float32) + 0.5 - 0.5 * ky_count) / (0.5 * ky_count)
    zero_col = jnp.zeros_like(distribution[:, :, :1])
    from_low = jnp.concatenate([zero_col, distribution[:, :, :-1]], axis=2)
    from_high = jnp.concatenate([distribution[:, :, 1:], zero_col], axis=2)
    upstream_y = jnp.where(upward[None, :, None, None], from_low, from_high)
    drift_y = -jnp.abs(vertical)[None, :, None, None] * (distribution - upstream_y)
    relaxation = relax_rate[:, None, :, None] * (
        density[:, None, :, None] * equilibrium[None, :, None, :] - distribution
    )
    base = distribution + STEP * (drift_x + drift_y + relaxation)
    wigner, base = lax.optimization_barrier((wigner, base))
    return base + STEP * wigner


def solution(mesh):
    return jax.shard_map(
        shards,
        mesh=mesh,
        in_specs=(
            P("space", "ky", None, None),
            P("space", None),
            P(),
            P(),
            P("ky", None),
            P(),
            P(),
        ),
        out_specs=P("space", "ky", None, None),
        check_vma=False,
    )
```
